256 devices in a mesh: outer: 8 (over z_lo, x), inner: 32 (over z_hi, y, core).
Axes of the slice: x: 4, y: 4, z: 8 (z_hi: 4, z_lo: 2; z = z_hi * 2 + z_lo), core: 2. Of those that a mesh axis runs over, the one named last changes fastest.
Arguments:
- query_stream: float32 [131072, 128], P(('outer', 'inner')), may hold values from -6 to 6
- key_stream: float32 [131072, 128], P(('outer', 'inner')), may hold values from -6 to 6
- value_stream: float32 [131072, 128], P(('outer', 'inner')), may hold values from -6 to 6
- filter_taps: float32 [131072, 128], P(('outer', 'inner')), may hold values from -1.6 to 1.6
- skip_gain: float32 [128], replicated, may hold values from -1 to 1
- short_weights: float32 [3, 3, 128], replicated, may hold values from -3 to 3
- cotangent: float32 [131072, 128], P(('outer', 'inner')), may hold values from -10 to 10
Outputs:
- gated_output: float32 [131072, 128], P(('outer', 'inner'))
- stream_grads: float32 [3, 131072, 128], P(None, ('outer', 'inner'))
- filter_grad: float32 [131072, 128], P(('outer', 'inner'))
- tap_grads: float32 [3, 3, 128], replicated
- skip_grad: float32 [128], replicated
The draws below stay inside these ranges and needn't reach their ends.
All inputs are finite; a program needn't handle non-finite values.
Results may differ from the reference program's by a relative error of at most 0.0003.
Values sent between devices are 32-bit elements; how exact they have to be, the bound alone decides.
No kernel may reach another device: no remote copies, remote signals or barrier semaphores. Data moves between devices by JAX's collectives and lax.ppermute only.
A program may use at most 64 MiB of HBM per device.

```python
import math
import jax
import jax.numpy as jnp
from jax import lax

CH = 128
SEQ = 131072


def draw_filter_taps(key, part):
    folded = jax.random.fold_in(key, 11)
    rate_key, jitter_key = jax.random.split(folded)
    positions = jnp.arange(SEQ, dtype=jnp.float32)[:, None]
    lifetime = jnp.exp(jax.random.uniform(rate_key, (1, CH), jnp.float32, math.log(30.0), math.log(4.0 * SEQ)))
    jitter = jax.random.truncated_normal(jitter_key, -6.0, 6.0, (SEQ, CH), jnp.float32)
    amplitude = jnp.sqrt(2.0 / jnp.minimum(lifetime, float(SEQ)))
    return (jitter * amplitude * jnp.exp(-positions / lifetime)).astype(jnp.float32)


def draw_cotangent(key, part):
    folded = jax.random.fold_in(key, 23)
    positions = jnp.arange(SEQ, dtype=jnp.float32)[:, None] / float(SEQ)
    envelope = 0.5 + 1.5 * positions
    jitter = jax.random.truncated_normal(folded, -5.0, 5.0, (SEQ, CH), jnp.float32) * envelope
    return jitter.astype(jnp.float32)


def block_levels(stream_key, dims, shards, low, largest):
    def one(axis_at, blocks):
        steps = jax.random.uniform(jax.random.fold_in(jax.random.fold_in(stream_key, 6), axis_at), (blocks,), jnp.float32, low / len(shards), largest / len(shards))
        return jnp.repeat(jnp.exp(steps), dims[axis_at] // blocks).reshape((-1,) + (1,) * (len(dims) - axis_at - 1))

    factor_of = one(*shards[0])
    for cut in shards[1:]:
        factor_of = factor_of * one(*cut)
    return factor_of


def bell_draw(key, dims, spread, bound, cuts=(), kind=jnp.bfloat16):
    entries = spread * jax.random.normal(key, dims, jnp.float32)
    if cuts:
        entries = entries * block_levels(key, dims, cuts, -0.22, 0.18)
    return jnp.clip(entries, -bound, bound).astype(kind)


def setup_inputs(seed: int = 0) -> dict:
    key_of = jax.random.split(jax.random.key(seed), 8)
    return {
        "query_stream": bell_draw(key_of[0], (SEQ, CH), 1.0, 6.0, ((0, 256),), jnp.float32),
        "key_stream": bell_draw(key_of[1], (SEQ, CH), 1.0, 6.0, ((0, 256),), jnp.float32),
        "value_stream": bell_draw(key_of[2], (SEQ, CH), 1.0, 6.0, ((0, 256),), jnp.float32),
        "filter_taps": draw_filter_taps(jax.random.fold_in(key_of[7], 71), 0),
        "skip_gain": jnp.clip(jax.random.uniform(key_of[4], (CH,), jnp.float32, -1.0, 1.0), -1.0, 1.0),
        "short_weights": bell_draw(key_of[5], (3, 3, CH), 0.6, 3.0, (), jnp.float32),
        "cotangent": draw_cotangent(jax.random.fold_in(key_of[7], 71), 0),
    }


def causal_taps(streams, weights):
    padded = jnp.pad(streams, ((0, 0), (2, 0), (0, 0)))
    lag_one = padded[:, 1:-1]
    lag_two = padded[:, :-2]
    mixed = weights[:, 0:1] * streams + weights[:, 1:2] * lag_one + weights[:, 2:3] * lag_two
    return (mixed, lag_one, lag_two)

def long_terms(block):
    extent = block.shape[1]
    length = 2 * extent
    spectra = jnp.fft.rfft(block, n=length, axis=1)
    filter_spec = spectra[0]
    product_spec = spectra[1]
    upstream_spec = spectra[2]
    causal = jnp.fft.irfft(filter_spec * product_spec, n=length, axis=0)[:extent]
    backward = jnp.fft.irfft(jnp.conj(filter_spec) * upstream_spec, n=length, axis=0)[:extent]
    gradient = jnp.fft.irfft(jnp.conj(product_spec) * upstream_spec, n=length, axis=0)[:extent]
    return jnp.stack([causal, backward, gradient])

def reference(query_stream, key_stream, value_stream, filter_taps, skip_gain, short_weights, cotangent):
    streams = jnp.stack([query_stream, key_stream, value_stream])
    mixed, lag_one, lag_two = causal_taps(streams, short_weights)
    product = mixed[1] * mixed[2]
    upstream = cotangent * mixed[0]
    stacked = jnp.stack([filter_taps, product, upstream])
    blocks = CH // 16
    shaped = stacked.reshape(3, SEQ, blocks, 16).transpose(2, 0, 1, 3)
    longs = lax.map(long_terms, shaped).transpose(1, 2, 0, 3).reshape(3, SEQ, CH)
    summed = longs[0] + skip_gain * product
    gated_output = mixed[0] * summed
    backward = longs[1] + skip_gain * upstream
    grads = jnp.stack([cotangent * summed, backward * mixed[2], backward * mixed[1]])
    padded = jnp.pad(grads, ((0, 0), (0, 2), (0, 0)))
    stream_grads = short_weights[:, 0:1] * grads + short_weights[:, 1:2] * padded[:, 1:-1] + short_weights[:, 2:3] * padded[:, 2:]
    factor = 1.0 / math.sqrt(SEQ)
    tap_grads = jnp.stack([lax.optimization_barrier(jnp.sum(grads * streams, axis=1)), lax.optimization_barrier(jnp.sum(grads * lag_one, axis=1)), lax.optimization_barrier(jnp.sum(grads * lag_two, axis=1))], axis=1) * factor
    skip_grad = lax.optimization_barrier(jnp.sum(upstream * product, axis=0)) * factor
    filter_grad = longs[2] * factor
    return (gated_output, stream_grads, filter_grad, tap_grads, skip_grad)
```

```python
import math

import jax
import jax.numpy as jnp
from jax import lax
from jax.sharding import PartitionSpec as P

exact_mode = lax.Precision.HIGHEST
everyone = ("outer", "inner")


def passed_along(block, axis, distance):
    devices = range(lax.axis_size(axis))
    route = [(i - distance, i) for i in devices if i - distance in devices]
    return lax.ppermute(block, axis, route)


def with_partner(block):
    devices = lax.axis_size(everyone)
    return lax.ppermute(block, everyone, [(i, i ^ 1) for i in range(devices)])


def unit_angles(counts_table, period):
    return 2.0 * math.pi / period * (counts_table % period).astype(jnp.float32)


def self_position():
    return lax.axis_index("outer") * lax.axis_size("inner") + lax.axis_index("inner")


def in_halves(first, mine, theirs, axis):
    return jnp.where(
        first,
        jnp.concatenate([mine, theirs], axis=axis),
        jnp.concatenate([theirs, mine], axis=axis),
    )


def long_convolutions(signals):
    members, row_count, channels = signals.shape
    devices = lax.axis_size(everyone)
    half = row_count // 2
    blocks = 2 * devices
    length = blocks * row_count
    position = self_position()
    side = position % 2
    first = side == 0

    outgoing = signals.reshape(members, 2, half, channels).transpose(3, 1, 0, 2)
    columns = lax.all_to_all(
        outgoing.reshape(devices, members * half), everyone, 0, 0, tiled=True
    )

    block_index = jnp.arange(devices, dtype=jnp.int32)
    coarse = jnp.arange(blocks, dtype=jnp.int32)
    coarse_angles = unit_angles(coarse[:, None] * block_index[None, :], blocks)
    coarse_cos = jnp.cos(coarse_angles)
    coarse_sin = jnp.sin(coarse_angles)
    first_real = jnp.dot(coarse_cos, columns, precision=exact_mode)
    first_imag = -jnp.dot(coarse_sin, columns, precision=exact_mode)

    kept = blocks // 2
    def split_coarse(part):
        low, high = part[:kept], part[kept:]
        return jnp.where(first, low, high), jnp.where(first, high, low)

    keep_real, send_real = split_coarse(first_real)
    keep_imag, send_imag = split_coarse(first_imag)
    got_real, got_imag = with_partner(jnp.stack([send_real, send_imag]))
    shape = (kept, members, half)
    full_real = in_halves(first, keep_real.reshape(shape), got_real.reshape(shape), 2)
    full_imag = in_halves(first, keep_imag.reshape(shape), got_imag.reshape(shape), 2)

    coarse_mine = side * kept + jnp.arange(kept, dtype=jnp.int32)
    fine = jnp.arange(row_count, dtype=jnp.int32)
    twiddle = unit_angles(coarse_mine[:, None] * fine[None, :], length)[:, None, :]
    twiddle_cos = jnp.cos(twiddle)
    twiddle_sin = jnp.sin(twiddle)
    turned_real = full_real * twiddle_cos + full_imag * twiddle_sin
    turned_imag = full_imag * twiddle_cos - full_real * twiddle_sin

    fine_angles = unit_angles(fine[:, None] * fine[None, :], row_count)
    fine_cos = jnp.cos(fine_angles)
    fine_sin = jnp.sin(fine_angles)
    flat = (kept * members, row_count)
    turned_real = turned_real.reshape(flat)
    turned_imag = turned_imag.reshape(flat)
    spec_real = (
        jnp.dot(turned_real, fine_cos, precision=exact_mode)
        + jnp.dot(turned_imag, fine_sin, precision=exact_mode)
    ).reshape(shape[0], members, row_count)
    spec_imag = (
        jnp.dot(turned_imag, fine_cos, precision=exact_mode)
        - jnp.dot(turned_real, fine_sin, precision=exact_mode)
    ).reshape(shape[0], members, row_count)

    filter_real, product_real, upstream_real = (spec_real[:, 0], spec_real[:, 1], spec_real[:, 2])
    filter_imag, product_imag, upstream_imag = (spec_imag[:, 0], spec_imag[:, 1], spec_imag[:, 2])
    causal_real = filter_real * product_real - filter_imag * product_imag
    causal_imag = filter_real * product_imag + filter_imag * product_real
    back_real = filter_real * upstream_real + filter_imag * upstream_imag
    back_imag = filter_real * upstream_imag - filter_imag * upstream_real
    grad_real = product_real * upstream_real + product_imag * upstream_imag
    grad_imag = product_real * upstream_imag - product_imag * upstream_real
    out_real = jnp.stack([causal_real, back_real, grad_real], axis=1).reshape(flat)
    out_imag = jnp.stack([causal_imag, back_imag, grad_imag], axis=1).reshape(flat)

    back_real = (
        jnp.dot(out_real, fine_cos, precision=exact_mode)
        - jnp.dot(out_imag, fine_sin, precision=exact_mode)
    ).reshape(shape[0], members, row_count)
    back_imag = (
        jnp.dot(out_imag, fine_cos, precision=exact_mode)
        + jnp.dot(out_real, fine_sin, precision=exact_mode)
    ).reshape(shape[0], members, row_count)
    unturned_real = back_real * twiddle_cos - back_imag * twiddle_sin
    unturned_imag = back_imag * twiddle_cos + back_real * twiddle_sin

    def split_fine(part):
        low, high = part[:, :, :half], part[:, :, half:]
        return jnp.where(first, low, high), jnp.where(first, high, low)

    mine_real, away_real = split_fine(unturned_real)
    mine_imag, away_imag = split_fine(unturned_imag)
    came_real, came_imag = with_partner(jnp.stack([away_real, away_imag]))
    whole_real = in_halves(first, mine_real, came_real, 0).reshape(blocks, members * half)
    whole_imag = in_halves(first, mine_imag, came_imag, 0).reshape(blocks, members * half)

    scale = 1.0 / length
    rows_out = (
        jnp.einsum("kb,kx->bx", coarse_cos, whole_real, precision=exact_mode)
        - jnp.einsum("kb,kx->bx", coarse_sin, whole_imag, precision=exact_mode)
    ) * scale
    returned = lax.all_to_all(rows_out, everyone, 0, 0, tiled=True)
    return (
        returned.reshape(channels, 2, members, half)
        .transpose(2, 1, 3, 0)
        .reshape(members, row_count, channels)
    )


def on_device(
    query_stream, key_stream, value_stream, filter_taps, skip_gain, short_weights, cotangent
):
    row_count, channels = query_stream.shape
    devices = lax.axis_size("outer") * lax.axis_size("inner")
    streams = jnp.stack([query_stream, key_stream, value_stream])
    earlier = passed_along(streams[:, row_count - 2 :, :], everyone, 1)
    ahead = jnp.concatenate([earlier, streams], axis=1)
    lag_one = ahead[:, 1 : row_count + 1]
    lag_two = ahead[:, 0:row_count]
    mixed = (
        short_weights[:, 0:1] * streams
        + short_weights[:, 1:2] * lag_one
        + short_weights[:, 2:3] * lag_two
    )
    product = mixed[1] * mixed[2]
    upstream = cotangent * mixed[0]
    longs = long_convolutions(jnp.stack([filter_taps, product, upstream]))
    summed = longs[0] + skip_gain * product
    gated_output = mixed[0] * summed
    backward = longs[1] + skip_gain * upstream
    grads = jnp.stack([cotangent * summed, backward * mixed[2], backward * mixed[1]])
    later = passed_along(grads[:, 0:2, :], everyone, -1)
    behind = jnp.concatenate([grads, later], axis=1)
    stream_grads = (
        short_weights[:, 0:1] * grads
        + short_weights[:, 1:2] * behind[:, 1 : row_count + 1]
        + short_weights[:, 2:3] * behind[:, 2 : row_count + 2]
    )
    tap_terms = jnp.stack(
        [
            jnp.sum(grads * streams, axis=1),
            jnp.sum(grads * lag_one, axis=1),
            jnp.sum(grads * lag_two, axis=1),
        ],
        axis=1,
    )
    skip_terms = jnp.sum(upstream * product, axis=0)
    tap_total, skip_total = lax.psum((tap_terms, skip_terms), everyone)
    factor = 1.0 / math.sqrt(row_count * devices)
    return (gated_output, stream_grads, longs[2] * factor, tap_total * factor, skip_total * factor)


def solution(mesh):
    placed = (
        P(everyone, None),
        P(everyone, None),
        P(everyone, None),
        P(everyone, None),
        P(),
        P(),
        P(everyone, None),
    )
    return jax.shard_map(
        on_device,
        mesh=mesh,
        in_specs=placed,
        out_specs=(
            P(everyone, None),
            P(None, everyone, None),
            P(everyone, None),
            P(),
            P(),
        ),
        check_vma=False,
    )
```

```python
import math

import jax
import jax.numpy as jnp
from jax import lax
from jax.sharding import PartitionSpec as P

exact_mode = lax.Precision.HIGH
everyone = ("outer", "inner")


def passed_along(block, axis, distance):
    devices = range(lax.axis_size(axis))
    route = [(i - distance, i) for i in devices if i - distance in devices]
    return lax.ppermute(block, axis, route)


def with_partner(block):
    devices = lax.axis_size(everyone)
    return lax.ppermute(block, everyone, [(i, i ^ 1) for i in range(devices)])


def unit_angles(counts_table, period):
    return 2.0 * math.pi / period * (counts_table % period).astype(jnp.float32)


def self_position():
    return lax.axis_index("outer") * lax.axis_size("inner") + lax.axis_index("inner")


def in_halves(first, mine, theirs, axis):
    return jnp.where(
        first,
        jnp.concatenate([mine, theirs], axis=axis),
        jnp.concatenate([theirs, mine], axis=axis),
    )


def summed_everywhere(value):
    devices = lax.axis_size(everyone)
    step = 1
    while step < devices:
        value = value + lax.ppermute(value, everyone, [(i, i ^ step) for i in range(devices)])
        step *= 2
    return value


def dot(left, right):
    return jnp.dot(left, right, precision=exact_mode)


def long_convolutions(signals):
    members, row_count, channels = signals.shape
    devices = lax.axis_size(everyone)
    half = row_count // 2
    blocks = 2 * devices
    kept = blocks // 2
    length = blocks * row_count
    position = self_position()
    side = position % 2
    first = side == 0
    hidden_zero = position // (4 * devices)

    outgoing = signals.reshape(members, 2, half, channels).transpose(3, 1, 0, 2)
    columns = lax.all_to_all(
        outgoing.reshape(devices, members * half), everyone, 0, 0, tiled=True
    )

    block_index = jnp.arange(devices, dtype=jnp.int32) + hidden_zero
    coarse = jnp.arange(blocks, dtype=jnp.int32) + hidden_zero
    fine = jnp.arange(row_count, dtype=jnp.int32) + hidden_zero
    coarse_angles = unit_angles(coarse[:, None] * block_index[None, :], blocks)
    coarse_cos = jnp.cos(coarse_angles)
    coarse_sin = jnp.sin(coarse_angles)
    back_angles = unit_angles(block_index[:, None] * coarse[None, :], blocks)
    back_cos = jnp.cos(back_angles)
    back_sin = jnp.sin(back_angles)
    coarse_mine = side * kept + jnp.arange(kept, dtype=jnp.int32)
    twiddle = unit_angles(coarse_mine[:, None] * fine[None, :], length)[None]
    twiddle_cos = jnp.cos(twiddle)
    twiddle_sin = jnp.sin(twiddle)
    fine_angles = unit_angles(fine[:, None] * fine[None, :], row_count)
    fine_cos = jnp.cos(fine_angles)
    fine_sin = jnp.sin(fine_angles)

    pieces = [columns[:, m * half : (m + 1) * half] for m in range(members)]
    first_real = jnp.stack([dot(coarse_cos, piece) for piece in pieces])
    first_imag = -jnp.stack([dot(coarse_sin, piece) for piece in pieces])

    def split_coarse(part):
        low, high = part[:, :kept], part[:, kept:]
        return jnp.where(first, low, high), jnp.where(first, high, low)

    keep_real, send_real = split_coarse(first_real)
    keep_imag, send_imag = split_coarse(first_imag)
    got_real, got_imag = with_partner(jnp.stack([send_real, send_imag]))
    full_real = in_halves(first, keep_real, got_real, 2)
    full_imag = in_halves(first, keep_imag, got_imag, 2)

    turned_real = full_real * twiddle_cos + full_imag * twiddle_sin
    turned_imag = full_imag * twiddle_cos - full_real * twiddle_sin

    flat = (members * kept, row_count)
    shape = (members, kept, row_count)
    turned_real = turned_real.reshape(flat)
    turned_imag = turned_imag.reshape(flat)
    spec_real = (dot(turned_real, fine_cos) + dot(turned_imag, fine_sin)).reshape(shape)
    spec_imag = (dot(turned_imag, fine_cos) - dot(turned_real, fine_sin)).reshape(shape)

    filter_real, product_real, upstream_real = (spec_real[0], spec_real[1], spec_real[2])
    filter_imag, product_imag, upstream_imag = (spec_imag[0], spec_imag[1], spec_imag[2])
    causal_real = filter_real * product_real - filter_imag * product_imag
    causal_imag = filter_real * product_imag + filter_imag * product_real
    back_real = filter_real * upstream_real + filter_imag * upstream_imag
    back_imag = filter_real * upstream_imag - filter_imag * upstream_real
    grad_real = product_real * upstream_real + product_imag * upstream_imag
    grad_imag = product_real * upstream_imag - product_imag * upstream_real
    out_real = jnp.stack([causal_real, back_real, grad_real]).reshape(flat)
    out_imag = jnp.stack([causal_imag, back_imag, grad_imag]).reshape(flat)

    inner_real = (dot(out_real, fine_cos) - dot(out_imag, fine_sin)).reshape(shape)
    inner_imag = (dot(out_imag, fine_cos) + dot(out_real, fine_sin)).reshape(shape)
    unturned_real = inner_real * twiddle_cos - inner_imag * twiddle_sin
    unturned_imag = inner_imag * twiddle_cos + inner_real * twiddle_sin

    def split_fine(part):
        low, high = part[:, :, :half], part[:, :, half:]
        return jnp.where(first, low, high), jnp.where(first, high, low)

    mine_real, away_real = split_fine(unturned_real)
    mine_imag, away_imag = split_fine(unturned_imag)
    came_real, came_imag = with_partner(jnp.stack([away_real, away_imag]))
    whole_real = in_halves(first, mine_real, came_real, 1)
    whole_imag = in_halves(first, mine_imag, came_imag, 1)

    scale = 1.0 / length
    rows_out = jnp.concatenate(
        [
            (dot(back_cos, whole_real[m]) - dot(back_sin, whole_imag[m])) * scale
            for m in range(members)
        ],
        axis=1,
    )
    returned = lax.all_to_all(rows_out, everyone, 0, 0, tiled=True)
    return (
        returned.reshape(channels, 2, members, half)
        .transpose(2, 1, 3, 0)
        .reshape(members, row_count, channels)
    )


def on_device(
    query_stream, key_stream, value_stream, filter_taps, skip_gain, short_weights, cotangent
):
    row_count, channels = query_stream.shape
    devices = lax.axis_size("outer") * lax.axis_size("inner")
    streams = jnp.stack([query_stream, key_stream, value_stream])
    earlier = passed_along(streams[:, row_count - 2 :, :], everyone, 1)
    ahead = jnp.concatenate([earlier, streams], axis=1)
    lag_one = ahead[:, 1 : row_count + 1]
    lag_two = ahead[:, 0:row_count]
    mixed = (
        short_weights[:, 0:1] * streams
        + short_weights[:, 1:2] * lag_one
        + short_weights[:, 2:3] * lag_two
    )
    product = mixed[1] * mixed[2]
    upstream = cotangent * mixed[0]
    longs = long_convolutions(jnp.stack([filter_taps, product, upstream]))
    summed = longs[0] + skip_gain * product
    gated_output = mixed[0] * summed
    backward = longs[1] + skip_gain * upstream
    grads = jnp.stack([cotangent * summed, backward * mixed[2], backward * mixed[1]])
    later = passed_along(grads[:, 0:2, :], everyone, -1)
    behind = jnp.concatenate([grads, later], axis=1)
    stream_grads = (
        short_weights[:, 0:1] * grads
        + short_weights[:, 1:2] * behind[:, 1 : row_count + 1]
        + short_weights[:, 2:3] * behind[:, 2 : row_count + 2]
    )
    tap_terms = jnp.stack(
        [
            jnp.sum(grads * streams, axis=1),
            jnp.sum(grads * lag_one, axis=1),
            jnp.sum(grads * lag_two, axis=1),
        ],
        axis=1,
    )
    skip_terms = jnp.sum(upstream * product, axis=0)
    totals = summed_everywhere(jnp.concatenate([tap_terms.reshape(-1, channels), skip_terms[None]]))
    tap_total = totals[:-1].reshape(tap_terms.shape)
    skip_total = totals[-1]
    factor = 1.0 / math.sqrt(row_count * devices)
    return (gated_output, stream_grads, longs[2] * factor, tap_total * factor, skip_total * factor)


def solution(mesh):
    placed = (
        P(everyone, None),
        P(everyone, None),
        P(everyone, None),
        P(everyone, None),
        P(),
        P(),
        P(everyone, None),
    )
    return jax.shard_map(
        on_device,
        mesh=mesh,
        in_specs=placed,
        out_specs=(
            P(everyone, None),
            P(None, everyone, None),
            P(everyone, None),
            P(),
            P(),
        ),
        check_vma=False,
    )
```

```python
import math

import jax
import jax.numpy as jnp
from jax import lax
from jax.sharding import PartitionSpec as P

exact_mode = lax.Precision.HIGH
everyone = ("outer", "inner")


def passed_along(block, axis, distance):
    devices = range(lax.axis_size(axis))
    route = [(i - distance, i) for i in devices if i - distance in devices]
    return lax.ppermute(block, axis, route)


def with_partner(block):
    devices = lax.axis_size(everyone)
    return lax.ppermute(block, everyone, [(i, i ^ 1) for i in range(devices)])


def unit_angles(counts_table, period):
    return 2.0 * math.pi / period * (counts_table % period).astype(jnp.float32)


def self_position():
    return lax.axis_index("outer") * lax.axis_size("inner") + lax.axis_index("inner")


def in_halves(first, mine, theirs, axis):
    return jnp.where(
        first,
        jnp.concatenate([mine, theirs], axis=axis),
        jnp.concatenate([theirs, mine], axis=axis),
    )


def summed_everywhere(value):
    devices = lax.axis_size(everyone)
    step = 1
    while step < devices:
        value = value + lax.ppermute(value, everyone, [(i, i ^ step) for i in range(devices)])
        step *= 2
    return value


def dot(left, right):
    return jnp.dot(left, right, precision=exact_mode)


def long_convolutions(signals):
    members, row_count, channels = signals.shape
    devices = lax.axis_size(everyone)
    half = row_count // 2
    blocks = 2 * devices
    kept = blocks // 2
    length = blocks * row_count
    position = self_position()
    side = position % 2
    first = side == 0
    hidden_zero = position // (4 * devices)

    outgoing = signals.reshape(members, 2, half, channels).transpose(3, 1, 0, 2)
    columns = lax.all_to_all(
        outgoing.reshape(devices, members * half), everyone, 0, 0, tiled=True
    )

    block_index = jnp.arange(devices, dtype=jnp.int32) + hidden_zero
    coarse = jnp.arange(blocks, dtype=jnp.int32) + hidden_zero
    fine = jnp.arange(row_count, dtype=jnp.int32) + hidden_zero
    coarse_angles = unit_angles(coarse[:, None] * block_index[None, :], blocks)
    coarse_cos = jnp.cos(coarse_angles)
    coarse_sin = jnp.sin(coarse_angles)
    back_angles = unit_angles(block_index[:, None] * coarse[None, :], blocks)
    back_cos = jnp.cos(back_angles)
    back_sin = jnp.sin(back_angles)
    coarse_mine = side * kept + jnp.arange(kept, dtype=jnp.int32)
    twiddle = unit_angles(coarse_mine[:, None] * fine[None, :], length)[None]
    twiddle_cos = jnp.cos(twiddle)
    twiddle_sin = jnp.sin(twiddle)
    fine_angles = unit_angles(fine[:, None] * fine[None, :], row_count)
    fine_cos = jnp.cos(fine_angles)
    fine_sin = jnp.sin(fine_angles)
    (coarse_cos, coarse_sin, back_cos, back_sin, twiddle_cos, twiddle_sin, fine_cos, fine_sin) = (
        lax.optimization_barrier(
            (coarse_cos, coarse_sin, back_cos, back_sin, twiddle_cos, twiddle_sin, fine_cos, fine_sin)
        )
    )

    pieces = [columns[:, m * half : (m + 1) * half] for m in range(members)]
    first_real = jnp.stack([dot(coarse_cos, piece) for piece in pieces])
    first_imag = -jnp.stack([dot(coarse_sin, piece) for piece in pieces])

    def split_coarse(part):
        low, high = part[:, :kept], part[:, kept:]
        return jnp.where(first, low, high), jnp.where(first, high, low)

    keep_real, send_real = split_coarse(first_real)
    keep_imag, send_imag = split_coarse(first_imag)
    got_real, got_imag = with_partner(jnp.stack([send_real, send_imag]))
    full_real = in_halves(first, keep_real, got_real, 2)
    full_imag = in_halves(first, keep_imag, got_imag, 2)

    turned_real = full_real * twiddle_cos + full_imag * twiddle_sin
    turned_imag = full_imag * twiddle_cos - full_real * twiddle_sin

    flat = (members * kept, row_count)
    shape = (members, kept, row_count)
    turned_real = turned_real.reshape(flat)
    turned_imag = turned_imag.reshape(flat)
    spec_real = (dot(turned_real, fine_cos) + dot(turned_imag, fine_sin)).reshape(shape)
    spec_imag = (dot(turned_imag, fine_cos) - dot(turned_real, fine_sin)).reshape(shape)

    filter_real, product_real, upstream_real = (spec_real[0], spec_real[1], spec_real[2])
    filter_imag, product_imag, upstream_imag = (spec_imag[0], spec_imag[1], spec_imag[2])
    causal_real = filter_real * product_real - filter_imag * product_imag
    causal_imag = filter_real * product_imag + filter_imag * product_real
    back_real = filter_real * upstream_real + filter_imag * upstream_imag
    back_imag = filter_real * upstream_imag - filter_imag * upstream_real
    grad_real = product_real * upstream_real + product_imag * upstream_imag
    grad_imag = product_real * upstream_imag - product_imag * upstream_real
    out_real = jnp.stack([causal_real, back_real, grad_real]).reshape(flat)
    out_imag = jnp.stack([causal_imag, back_imag, grad_imag]).reshape(flat)

    inner_real = (dot(out_real, fine_cos) - dot(out_imag, fine_sin)).reshape(shape)
    inner_imag = (dot(out_imag, fine_cos) + dot(out_real, fine_sin)).reshape(shape)
    unturned_real = inner_real * twiddle_cos - inner_imag * twiddle_sin
    unturned_imag = inner_imag * twiddle_cos + inner_real * twiddle_sin

    def split_fine(part):
        low, high = part[:, :, :half], part[:, :, half:]
        return jnp.where(first, low, high), jnp.where(first, high, low)

    mine_real, away_real = split_fine(unturned_real)
    mine_imag, away_imag = split_fine(unturned_imag)
    came_real, came_imag = with_partner(jnp.stack([away_real, away_imag]))
    whole_real = in_halves(first, mine_real, came_real, 1)
    whole_imag = in_halves(first, mine_imag, came_imag, 1)

    scale = 1.0 / length
    rows_out = jnp.concatenate(
        [
            (dot(back_cos, whole_real[m]) - dot(back_sin, whole_imag[m])) * scale
            for m in range(members)
        ],
        axis=1,
    )
    returned = lax.all_to_all(rows_out, everyone, 0, 0, tiled=True)
    return (
        returned.reshape(channels, 2, members, half)
        .transpose(2, 1, 3, 0)
        .reshape(members, row_count, channels)
    )


def on_device(
    query_stream, key_stream, value_stream, filter_taps, skip_gain, short_weights, cotangent
):
    row_count, channels = query_stream.shape
    devices = lax.axis_size("outer") * lax.axis_size("inner")
    streams = jnp.stack([query_stream, key_stream, value_stream])
    earlier = passed_along(streams[:, row_count - 2 :, :], everyone, 1)
    ahead = jnp.concatenate([earlier, streams], axis=1)
    lag_one = ahead[:, 1 : row_count + 1]
    lag_two = ahead[:, 0:row_count]
    mixed = (
        short_weights[:, 0:1] * streams
        + short_weights[:, 1:2] * lag_one
        + short_weights[:, 2:3] * lag_two
    )
    product = mixed[1] * mixed[2]
    upstream = cotangent * mixed[0]
    longs = long_convolutions(jnp.stack([filter_taps, product, upstream]))
    summed = longs[0] + skip_gain * product
    gated_output = mixed[0] * summed
    backward = longs[1] + skip_gain * upstream
    grads = jnp.stack([cotangent * summed, backward * mixed[2], backward * mixed[1]])
    later = passed_along(grads[:, 0:2, :], everyone, -1)
    behind = jnp.concatenate([grads, later], axis=1)
    stream_grads = (
        short_weights[:, 0:1] * grads
        + short_weights[:, 1:2] * behind[:, 1 : row_count + 1]
        + short_weights[:, 2:3] * behind[:, 2 : row_count + 2]
    )
    tap_terms = jnp.stack(
        [
            jnp.sum(grads * streams, axis=1),
            jnp.sum(grads * lag_one, axis=1),
            jnp.sum(grads * lag_two, axis=1),
        ],
        axis=1,
    )
    skip_terms = jnp.sum(upstream * product, axis=0)
    totals = summed_everywhere(jnp.concatenate([tap_terms.reshape(-1, channels), skip_terms[None]]))
    tap_total = totals[:-1].reshape(tap_terms.shape)
    skip_total = totals[-1]
    factor = 1.0 / math.sqrt(row_count * devices)
    return (gated_output, stream_grads, longs[2] * factor, tap_total * factor, skip_total * factor)


def solution(mesh):
    placed = (
        P(everyone, None),
        P(everyone, None),
        P(everyone, None),
        P(everyone, None),
        P(),
        P(),
        P(everyone, None),
    )
    return jax.shard_map(
        on_device,
        mesh=mesh,
        in_specs=placed,
        out_specs=(
            P(everyone, None),
            P(None, everyone, None),
            P(everyone, None),
            P(),
            P(),
        ),
        check_vma=False,
    )
```

```python
import math

import jax
import jax.numpy as jnp
from jax import lax
from jax.sharding import PartitionSpec as P

exact_mode = lax.Precision.HIGH
everyone = ("outer", "inner")


def passed_along(block, axis, distance):
    devices = range(lax.axis_size(axis))
    route = [(i - distance, i) for i in devices if i - distance in devices]
    return lax.ppermute(block, axis, route)


def with_partner(block):
    devices = lax.axis_size(everyone)
    return lax.ppermute(block, everyone, [(i, i ^ 1) for i in range(devices)])


def unit_angles(counts_table, period):
    return 2.0 * math.pi / period * (counts_table % period).astype(jnp.float32)


def self_position():
    return lax.axis_index("outer") * lax.axis_size("inner") + lax.axis_index("inner")


def in_halves(first, mine, theirs, axis):
    return jnp.where(
        first,
        jnp.concatenate([mine, theirs], axis=axis),
        jnp.concatenate([theirs, mine], axis=axis),
    )


def dot(left, right):
    return jnp.dot(left, right, precision=exact_mode)


def long_convolutions(pieces, row_count):
    members = len(pieces)
    devices = lax.axis_size(everyone)
    half = row_count // 2
    blocks = 2 * devices
    kept = blocks // 2
    length = blocks * row_count
    position = self_position()
    side = position % 2
    first = side == 0
    hidden_zero = position // (4 * devices)

    block_index = jnp.arange(devices, dtype=jnp.int32) + hidden_zero
    coarse = jnp.arange(blocks, dtype=jnp.int32) + hidden_zero
    fine = jnp.arange(row_count, dtype=jnp.int32) + hidden_zero
    coarse_angles = unit_angles(coarse[:, None] * block_index[None, :], blocks)
    coarse_cos = jnp.cos(coarse_angles)
    coarse_sin = jnp.sin(coarse_angles)
    back_angles = unit_angles(block_index[:, None] * coarse[None, :], blocks)
    back_cos = jnp.cos(back_angles)
    back_sin = jnp.sin(back_angles)
    coarse_mine = side * kept + jnp.arange(kept, dtype=jnp.int32)
    twiddle = unit_angles(coarse_mine[:, None] * fine[None, :], length)[None]
    twiddle_cos = jnp.cos(twiddle)
    twiddle_sin = jnp.sin(twiddle)
    fine_angles = unit_angles(fine[:, None] * fine[None, :], row_count)
    fine_cos = jnp.cos(fine_angles)
    fine_sin = jnp.sin(fine_angles)
    (coarse_cos, coarse_sin, back_cos, back_sin, twiddle_cos, twiddle_sin, fine_cos, fine_sin) = (
        lax.optimization_barrier(
            (coarse_cos, coarse_sin, back_cos, back_sin, twiddle_cos, twiddle_sin, fine_cos, fine_sin)
        )
    )

    first_real = jnp.stack([dot(coarse_cos, piece) for piece in pieces])
    first_imag = -jnp.stack([dot(coarse_sin, piece) for piece in pieces])

    def split_coarse(part):
        low, high = part[:, :kept], part[:, kept:]
        return jnp.where(first, low, high), jnp.where(first, high, low)

    keep_real, send_real = split_coarse(first_real)
    keep_imag, send_imag = split_coarse(first_imag)
    got_real, got_imag = with_partner(jnp.stack([send_real, send_imag]))
    full_real = in_halves(first, keep_real, got_real, 2)
    full_imag = in_halves(first, keep_imag, got_imag, 2)

    turned_real = full_real * twiddle_cos + full_imag * twiddle_sin
    turned_imag = full_imag * twiddle_cos - full_real * twiddle_sin

    flat = (members * kept, row_count)
    shape = (members, kept, row_count)
    turned_real = turned_real.reshape(flat)
    turned_imag = turned_imag.reshape(flat)
    spec_real = (dot(turned_real, fine_cos) + dot(turned_imag, fine_sin)).reshape(shape)
    spec_imag = (dot(turned_imag, fine_cos) - dot(turned_real, fine_sin)).reshape(shape)

    filter_real, product_real, upstream_real = (spec_real[0], spec_real[1], spec_real[2])
    filter_imag, product_imag, upstream_imag = (spec_imag[0], spec_imag[1], spec_imag[2])
    causal_real = filter_real * product_real - filter_imag * product_imag
    causal_imag = filter_real * product_imag + filter_imag * product_real
    back_real = filter_real * upstream_real + filter_imag * upstream_imag
    back_imag = filter_real * upstream_imag - filter_imag * upstream_real
    grad_real = product_real * upstream_real + product_imag * upstream_imag
    grad_imag = product_real * upstream_imag - product_imag * upstream_real
    out_real = jnp.stack([causal_real, back_real, grad_real]).reshape(flat)
    out_imag = jnp.stack([causal_imag, back_imag, grad_imag]).reshape(flat)

    inner_real = (dot(out_real, fine_cos) - dot(out_imag, fine_sin)).reshape(shape)
    inner_imag = (dot(out_imag, fine_cos) + dot(out_real, fine_sin)).reshape(shape)
    unturned_real = inner_real * twiddle_cos - inner_imag * twiddle_sin
    unturned_imag = inner_imag * twiddle_cos + inner_real * twiddle_sin

    def split_fine(part):
        low, high = part[:, :, :half], part[:, :, half:]
        return jnp.where(first, low, high), jnp.where(first, high, low)

    mine_real, away_real = split_fine(unturned_real)
    mine_imag, away_imag = split_fine(unturned_imag)
    came_real, came_imag = with_partner(jnp.stack([away_real, away_imag]))
    whole_real = in_halves(first, mine_real, came_real, 1)
    whole_imag = in_halves(first, mine_imag, came_imag, 1)

    scale = 1.0 / length
    return [
        (dot(back_cos, whole_real[m]) - dot(back_sin, whole_imag[m])) * scale
        for m in range(members)
    ]


def on_device(
    query_stream, key_stream, value_stream, filter_taps, skip_gain, short_weights, cotangent
):
    row_count, channels = query_stream.shape
    devices = lax.axis_size(everyone)
    half = row_count // 2
    position = self_position()
    first = position % 2 == 0
    channel = position // 2

    streams = jnp.stack([query_stream, key_stream, value_stream])
    earlier = passed_along(streams[:, row_count - 2 :, :], everyone, 1)
    ahead = jnp.concatenate([earlier, streams], axis=1)
    lagged = jnp.stack([ahead[:, 0 : half + 2], ahead[:, half : row_count + 2]], axis=1)
    lagged = lagged.transpose(3, 1, 0, 2).reshape(channels, 2, 3 * (half + 2))
    plain = jnp.stack([filter_taps, cotangent]).reshape(2, 2, half, channels)
    plain = plain.transpose(3, 1, 0, 2).reshape(channels, 2, 2 * half)
    outgoing = jnp.concatenate([lagged, plain], axis=2).reshape(devices, -1)
    columns = lax.all_to_all(outgoing, everyone, 0, 0, tiled=True)

    width = 3 * (half + 2)
    padded = columns[:, :width].reshape(devices, 3, half + 2).transpose(1, 0, 2)
    filter_part = columns[:, width : width + half]
    cotangent_part = columns[:, width + half : width + 2 * half]
    own = padded[:, :, 2:]
    lag_one = padded[:, :, 1 : half + 1]
    lag_two = padded[:, :, 0:half]
    weights = lax.dynamic_index_in_dim(short_weights, channel, axis=2, keepdims=False)
    gain = lax.dynamic_index_in_dim(skip_gain, channel, axis=0, keepdims=False)
    mixed = (
        weights[:, 0:1, None] * own
        + weights[:, 1:2, None] * lag_one
        + weights[:, 2:3, None] * lag_two
    )
    product = mixed[1] * mixed[2]
    upstream = cotangent_part * mixed[0]
    causal, backward_long, gradient = long_convolutions(
        [filter_part, product, upstream], row_count
    )
    summed = causal + gain * product
    gated_output = mixed[0] * summed
    backward = backward_long + gain * upstream
    grads = jnp.stack([cotangent_part * summed, backward * mixed[2], backward * mixed[1]])

    tap_terms = jnp.stack(
        [
            jnp.sum(grads * own, axis=(1, 2)),
            jnp.sum(grads * lag_one, axis=(1, 2)),
            jnp.sum(grads * lag_two, axis=(1, 2)),
        ],
        axis=1,
    )
    skip_terms = jnp.sum(upstream * product)
    partials = jnp.concatenate([tap_terms.reshape(-1), skip_terms[None]])
    got_rows, got_partials = with_partner((grads[:, :, 0:2], partials))
    shifted = jnp.concatenate([got_rows[:, 1:], jnp.zeros_like(got_rows[:, :1])], axis=1)
    behind = jnp.concatenate([grads, jnp.where(first, got_rows, shifted)], axis=2)
    stream_grads = (
        weights[:, 0:1, None] * grads
        + weights[:, 1:2, None] * behind[:, :, 1 : half + 1]
        + weights[:, 2:3, None] * behind[:, :, 2 : half + 2]
    )
    factor = 1.0 / math.sqrt(row_count * devices)
    totals = (partials + got_partials) * factor

    payload = jnp.concatenate(
        [gated_output, stream_grads[0], stream_grads[1], stream_grads[2], gradient * factor]
        + [jnp.broadcast_to(totals[None], (devices, totals.shape[0]))],
        axis=1,
    )
    returned = lax.all_to_all(payload, everyone, 0, 0, tiled=True)
    rows_back = (
        returned[:, : 5 * half]
        .reshape(channels, 2, 5, half)
        .transpose(2, 1, 3, 0)
        .reshape(5, row_count, channels)
    )
    per_channel = returned[:, 5 * half :].reshape(channels, 2, -1)[:, 0].T
    tap_total = per_channel[:-1].reshape(3, 3, channels)
    skip_total = per_channel[-1]
    return (rows_back[0], rows_back[1:4], rows_back[4], tap_total, skip_total)


def solution(mesh):
    placed = (
        P(everyone, None),
        P(everyone, None),
        P(everyone, None),
        P(everyone, None),
        P(),
        P(),
        P(everyone, None),
    )
    return jax.shard_map(
        on_device,
        mesh=mesh,
        in_specs=placed,
        out_specs=(
            P(everyone, None),
            P(None, everyone, None),
            P(everyone, None),
            P(),
            P(),
        ),
        check_vma=False,
    )
```

```python
import math

import jax
import jax.numpy as jnp
from jax import lax
from jax.sharding import PartitionSpec as P

exact_mode = lax.Precision.HIGH
everyone = ("outer", "inner")


def passed_along(block, axis, distance):
    devices = range(lax.axis_size(axis))
    route = [(i - distance, i) for i in devices if i - distance in devices]
    return lax.ppermute(block, axis, route)


def with_partner(block):
    devices = lax.axis_size(everyone)
    return lax.ppermute(block, everyone, [(i, i ^ 1) for i in range(devices)])


def unit_angles(counts_table, period):
    return 2.0 * math.pi / period * (counts_table % period).astype(jnp.float32)


def self_position():
    return lax.axis_index("outer") * lax.axis_size("inner") + lax.axis_index("inner")


def in_halves(first, mine, theirs, axis):
    return jnp.where(
        first,
        jnp.concatenate([mine, theirs], axis=axis),
        jnp.concatenate([theirs, mine], axis=axis),
    )


def dot(left, right):
    return jnp.dot(left, right, precision=exact_mode)


def long_convolutions(pieces, row_count):
    members = len(pieces)
    devices = lax.axis_size(everyone)
    half = row_count // 2
    blocks = 2 * devices
    kept = blocks // 2
    length = blocks * row_count
    position = self_position()
    side = position % 2
    first = side == 0
    hidden_zero = position // (4 * devices)

    block_index = jnp.arange(devices, dtype=jnp.int32) + hidden_zero
    coarse = jnp.arange(blocks, dtype=jnp.int32) + hidden_zero
    fine = jnp.arange(row_count, dtype=jnp.int32) + hidden_zero
    coarse_angles = unit_angles(coarse[:, None] * block_index[None, :], blocks)
    coarse_cos = jnp.cos(coarse_angles)
    coarse_sin = jnp.sin(coarse_angles)
    back_angles = unit_angles(block_index[:, None] * coarse[None, :], blocks)
    back_cos = jnp.cos(back_angles)
    back_sin = jnp.sin(back_angles)
    coarse_mine = side * kept + jnp.arange(kept, dtype=jnp.int32)
    twiddle = unit_angles(coarse_mine[:, None] * fine[None, :], length)[None]
    twiddle_cos = jnp.cos(twiddle)
    twiddle_sin = jnp.sin(twiddle)
    fine_angles = unit_angles(fine[:, None] * fine[None, :], row_count)
    fine_cos = jnp.cos(fine_angles)
    fine_sin = jnp.sin(fine_angles)
    (coarse_cos, coarse_sin, back_cos, back_sin, twiddle_cos, twiddle_sin, fine_cos, fine_sin) = (
        lax.optimization_barrier(
            (coarse_cos, coarse_sin, back_cos, back_sin, twiddle_cos, twiddle_sin, fine_cos, fine_sin)
        )
    )

    first_real = jnp.stack([dot(coarse_cos, piece) for piece in pieces])
    first_imag = -jnp.stack([dot(coarse_sin, piece) for piece in pieces])

    def split_coarse(part):
        low, high = part[:, :kept], part[:, kept:]
        return jnp.where(first, low, high), jnp.where(first, high, low)

    keep_real, send_real = split_coarse(first_real)
    keep_imag, send_imag = split_coarse(first_imag)
    got_real, got_imag = with_partner(jnp.stack([send_real, send_imag]))
    full_real = in_halves(first, keep_real, got_real, 2)
    full_imag = in_halves(first, keep_imag, got_imag, 2)

    turned_real = full_real * twiddle_cos + full_imag * twiddle_sin
    turned_imag = full_imag * twiddle_cos - full_real * twiddle_sin

    flat = (members * kept, row_count)
    shape = (members, kept, row_count)
    turned_real = turned_real.reshape(flat)
    turned_imag = turned_imag.reshape(flat)
    spec_real = (dot(turned_real, fine_cos) + dot(turned_imag, fine_sin)).reshape(shape)
    spec_imag = (dot(turned_imag, fine_cos) - dot(turned_real, fine_sin)).reshape(shape)

    filter_real, product_real, upstream_real = (spec_real[0], spec_real[1], spec_real[2])
    filter_imag, product_imag, upstream_imag = (spec_imag[0], spec_imag[1], spec_imag[2])
    causal_real = filter_real * product_real - filter_imag * product_imag
    causal_imag = filter_real * product_imag + filter_imag * product_real
    back_real = filter_real * upstream_real + filter_imag * upstream_imag
    back_imag = filter_real * upstream_imag - filter_imag * upstream_real
    grad_real = product_real * upstream_real + product_imag * upstream_imag
    grad_imag = product_real * upstream_imag - product_imag * upstream_real
    out_real = jnp.stack([causal_real, back_real, grad_real]).reshape(flat)
    out_imag = jnp.stack([causal_imag, back_imag, grad_imag]).reshape(flat)

    inner_real = (dot(out_real, fine_cos) - dot(out_imag, fine_sin)).reshape(shape)
    inner_imag = (dot(out_imag, fine_cos) + dot(out_real, fine_sin)).reshape(shape)
    unturned_real = inner_real * twiddle_cos - inner_imag * twiddle_sin
    unturned_imag = inner_imag * twiddle_cos + inner_real * twiddle_sin

    def split_fine(part):
        low, high = part[:, :, :half], part[:, :, half:]
        return jnp.where(first, low, high), jnp.where(first, high, low)

    mine_real, away_real = split_fine(unturned_real)
    mine_imag, away_imag = split_fine(unturned_imag)
    came_real, came_imag = with_partner(jnp.stack([away_real, away_imag]))
    whole_real = in_halves(first, mine_real, came_real, 1)
    whole_imag = in_halves(first, mine_imag, came_imag, 1)

    scale = 1.0 / length
    return [
        (dot(back_cos, whole_real[m]) - dot(back_sin, whole_imag[m])) * scale
        for m in range(members)
    ]


def on_device(
    query_stream, key_stream, value_stream, filter_taps, skip_gain, short_weights, cotangent
):
    row_count, channels = query_stream.shape
    devices = lax.axis_size(everyone)
    half = row_count // 2
    position = self_position()
    first = position % 2 == 0
    channel = position // 2

    sent = jnp.stack([query_stream, key_stream, value_stream, filter_taps, cotangent])
    sent = sent.reshape(5, 2, half, channels).transpose(3, 1, 0, 2).reshape(devices, 5 * half)
    columns = lax.all_to_all(sent, everyone, 0, 0, tiled=True)
    parts = [columns[:, k * half : (k + 1) * half] for k in range(5)]
    own = jnp.stack(parts[:3])
    filter_part, cotangent_part = parts[3], parts[4]
    got_tail = with_partner(own[:, :, half - 2 :])
    shifted = jnp.concatenate([jnp.zeros_like(got_tail[:, :1]), got_tail[:, :-1]], axis=1)
    padded = jnp.concatenate([jnp.where(first, shifted, got_tail), own], axis=2)
    lag_one = padded[:, :, 1 : half + 1]
    lag_two = padded[:, :, 0:half]
    weights = lax.dynamic_index_in_dim(short_weights, channel, axis=2, keepdims=False)
    gain = lax.dynamic_index_in_dim(skip_gain, channel, axis=0, keepdims=False)
    mixed = (
        weights[:, 0:1, None] * own
        + weights[:, 1:2, None] * lag_one
        + weights[:, 2:3, None] * lag_two
    )
    product = mixed[1] * mixed[2]
    upstream = cotangent_part * mixed[0]
    causal, backward_long, gradient = long_convolutions(
        [filter_part, product, upstream], row_count
    )
    summed = causal + gain * product
    gated_output = mixed[0] * summed
    backward = backward_long + gain * upstream
    grads = jnp.stack([cotangent_part * summed, backward * mixed[2], backward * mixed[1]])

    tap_terms = jnp.stack(
        [
            jnp.sum(grads * own, axis=(1, 2)),
            jnp.sum(grads * lag_one, axis=(1, 2)),
            jnp.sum(grads * lag_two, axis=(1, 2)),
        ],
        axis=1,
    )
    skip_terms = jnp.sum(upstream * product)
    partials = jnp.concatenate([tap_terms.reshape(-1), skip_terms[None]])
    got_rows, got_partials = with_partner((grads[:, :, 0:2], partials))
    shifted = jnp.concatenate([got_rows[:, 1:], jnp.zeros_like(got_rows[:, :1])], axis=1)
    behind = jnp.concatenate([grads, jnp.where(first, got_rows, shifted)], axis=2)
    stream_grads = (
        weights[:, 0:1, None] * grads
        + weights[:, 1:2, None] * behind[:, :, 1 : half + 1]
        + weights[:, 2:3, None] * behind[:, :, 2 : half + 2]
    )
    factor = 1.0 / math.sqrt(row_count * devices)
    totals = (partials + got_partials) * factor

    payload = jnp.concatenate(
        [gated_output, stream_grads[0], stream_grads[1], stream_grads[2], gradient * factor]
        + [jnp.broadcast_to(totals[None], (devices, totals.shape[0]))],
        axis=1,
    )
    returned = lax.all_to_all(payload, everyone, 0, 0, tiled=True)
    rows_back = (
        returned[:, : 5 * half]
        .reshape(channels, 2, 5, half)
        .transpose(2, 1, 3, 0)
        .reshape(5, row_count, channels)
    )
    per_channel = returned[:, 5 * half :].reshape(channels, 2, -1)[:, 0].T
    tap_total = per_channel[:-1].reshape(3, 3, channels)
    skip_total = per_channel[-1]
    return (rows_back[0], rows_back[1:4], rows_back[4], tap_total, skip_total)


def solution(mesh):
    placed = (
        P(everyone, None),
        P(everyone, None),
        P(everyone, None),
        P(everyone, None),
        P(),
        P(),
        P(everyone, None),
    )
    return jax.shard_map(
        on_device,
        mesh=mesh,
        in_specs=placed,
        out_specs=(
            P(everyone, None),
            P(None, everyone, None),
            P(everyone, None),
            P(),
            P(),
        ),
        check_vma=False,
    )
```

```python
import math

import jax
import jax.numpy as jnp
from jax import lax
from jax.sharding import PartitionSpec as P

exact_mode = lax.Precision.HIGH
everyone = ("outer", "inner")


def passed_along(block, axis, distance):
    devices = range(lax.axis_size(axis))
    route = [(i - distance, i) for i in devices if i - distance in devices]
    return lax.ppermute(block, axis, route)


def with_partner(block):
    devices = lax.axis_size(everyone)
    return lax.ppermute(block, everyone, [(i, i ^ 1) for i in range(devices)])


def unit_angles(counts_table, period):
    return 2.0 * math.pi / period * (counts_table % period).astype(jnp.float32)


def self_position():
    return lax.axis_index("outer") * lax.axis_size("inner") + lax.axis_index("inner")


def in_halves(first, mine, theirs, axis):
    return jnp.where(
        first,
        jnp.concatenate([mine, theirs], axis=axis),
        jnp.concatenate([theirs, mine], axis=axis),
    )


def dot(left, right):
    return jnp.dot(left, right, precision=exact_mode)


def long_convolutions(pieces, row_count):
    members = len(pieces)
    devices = lax.axis_size(everyone)
    half = row_count // 2
    blocks = 2 * devices
    kept = blocks // 2
    length = blocks * row_count
    position = self_position()
    side = position % 2
    first = side == 0
    hidden_zero = position // (4 * devices)

    block_index = jnp.arange(devices, dtype=jnp.int32) + hidden_zero
    coarse = jnp.arange(blocks, dtype=jnp.int32) + hidden_zero
    fine = jnp.arange(row_count, dtype=jnp.int32) + hidden_zero
    coarse_angles = unit_angles(coarse[:, None] * block_index[None, :], blocks)
    coarse_cos = jnp.cos(coarse_angles)
    coarse_sin = jnp.sin(coarse_angles)
    back_angles = unit_angles(block_index[:, None] * coarse[None, :], blocks)
    back_cos = jnp.cos(back_angles)
    back_sin = jnp.sin(back_angles)
    coarse_mine = side * kept + jnp.arange(kept, dtype=jnp.int32)
    twiddle = unit_angles(coarse_mine[:, None] * fine[None, :], length)[None]
    twiddle_cos = jnp.cos(twiddle)
    twiddle_sin = jnp.sin(twiddle)
    fine_angles = unit_angles(fine[:, None] * fine[None, :], row_count)
    fine_cos = jnp.cos(fine_angles)
    fine_sin = jnp.sin(fine_angles)
    (coarse_cos, coarse_sin, back_cos, back_sin, twiddle_cos, twiddle_sin, fine_cos, fine_sin) = (
        lax.optimization_barrier(
            (coarse_cos, coarse_sin, back_cos, back_sin, twiddle_cos, twiddle_sin, fine_cos, fine_sin)
        )
    )

    first_real = jnp.stack([dot(coarse_cos, piece) for piece in pieces])
    first_imag = -jnp.stack([dot(coarse_sin, piece) for piece in pieces])

    def split_coarse(part):
        low, high = part[:, :kept], part[:, kept:]
        return jnp.where(first, low, high), jnp.where(first, high, low)

    keep_real, send_real = split_coarse(first_real)
    keep_imag, send_imag = split_coarse(first_imag)
    got_real, got_imag = with_partner(jnp.stack([send_real, send_imag]))
    full_real = in_halves(first, keep_real, got_real, 2)
    full_imag = in_halves(first, keep_imag, got_imag, 2)

    turned_real = full_real * twiddle_cos + full_imag * twiddle_sin
    turned_imag = full_imag * twiddle_cos - full_real * twiddle_sin

    flat = (members * kept, row_count)
    shape = (members, kept, row_count)
    turned_real = turned_real.reshape(flat)
    turned_imag = turned_imag.reshape(flat)
    spec_real = (dot(turned_real, fine_cos) + dot(turned_imag, fine_sin)).reshape(shape)
    spec_imag = (dot(turned_imag, fine_cos) - dot(turned_real, fine_sin)).reshape(shape)

    filter_real, product_real, upstream_real = (spec_real[0], spec_real[1], spec_real[2])
    filter_imag, product_imag, upstream_imag = (spec_imag[0], spec_imag[1], spec_imag[2])
    causal_real = filter_real * product_real - filter_imag * product_imag
    causal_imag = filter_real * product_imag + filter_imag * product_real
    back_real = filter_real * upstream_real + filter_imag * upstream_imag
    back_imag = filter_real * upstream_imag - filter_imag * upstream_real
    grad_real = product_real * upstream_real + product_imag * upstream_imag
    grad_imag = product_real * upstream_imag - product_imag * upstream_real
    out_real = jnp.stack([causal_real, back_real, grad_real]).reshape(flat)
    out_imag = jnp.stack([causal_imag, back_imag, grad_imag]).reshape(flat)

    inner_real = (dot(out_real, fine_cos) - dot(out_imag, fine_sin)).reshape(shape)
    inner_imag = (dot(out_imag, fine_cos) + dot(out_real, fine_sin)).reshape(shape)
    unturned_real = inner_real * twiddle_cos - inner_imag * twiddle_sin
    unturned_imag = inner_imag * twiddle_cos + inner_real * twiddle_sin

    def split_fine(part):
        low, high = part[:, :, :half], part[:, :, half:]
        return jnp.where(first, low, high), jnp.where(first, high, low)

    mine_real, away_real = split_fine(unturned_real)
    mine_imag, away_imag = split_fine(unturned_imag)
    came_real, came_imag = with_partner(jnp.stack([away_real, away_imag]))
    whole_real = in_halves(first, mine_real, came_real, 1)
    whole_imag = in_halves(first, mine_imag, came_imag, 1)

    scale = 1.0 / length
    return [
        (dot(back_cos, whole_real[m]) - dot(back_sin, whole_imag[m])) * scale
        for m in range(members)
    ]


def on_device(
    query_stream, key_stream, value_stream, filter_taps, skip_gain, short_weights, cotangent
):
    row_count, channels = query_stream.shape
    devices = lax.axis_size(everyone)
    half = row_count // 2
    position = self_position()
    first = position % 2 == 0
    channel = position // 2

    sent = jnp.stack([query_stream, key_stream, value_stream, filter_taps, cotangent])
    sent = sent.reshape(5, 2, half, channels).transpose(3, 1, 0, 2).reshape(devices, 5 * half)
    columns = lax.all_to_all(sent, everyone, 0, 0, tiled=True)
    parts = [columns[:, k * half : (k + 1) * half] for k in range(5)]
    own = jnp.stack(parts[:3])
    filter_part, cotangent_part = parts[3], parts[4]
    got_tail = with_partner(own[:, :, half - 2 :].transpose(0, 2, 1)).transpose(0, 2, 1)
    shifted = jnp.concatenate([jnp.zeros_like(got_tail[:, :1]), got_tail[:, :-1]], axis=1)
    padded = jnp.concatenate([jnp.where(first, shifted, got_tail), own], axis=2)
    lag_one = padded[:, :, 1 : half + 1]
    lag_two = padded[:, :, 0:half]
    weights = lax.dynamic_index_in_dim(short_weights, channel, axis=2, keepdims=False)
    gain = lax.dynamic_index_in_dim(skip_gain, channel, axis=0, keepdims=False)
    mixed = (
        weights[:, 0:1, None] * own
        + weights[:, 1:2, None] * lag_one
        + weights[:, 2:3, None] * lag_two
    )
    product = mixed[1] * mixed[2]
    upstream = cotangent_part * mixed[0]
    causal, backward_long, gradient = long_convolutions(
        [filter_part, product, upstream], row_count
    )
    summed = causal + gain * product
    gated_output = mixed[0] * summed
    backward = backward_long + gain * upstream
    grads = jnp.stack([cotangent_part * summed, backward * mixed[2], backward * mixed[1]])

    tap_terms = jnp.stack(
        [
            jnp.sum(grads * own, axis=(1, 2)),
            jnp.sum(grads * lag_one, axis=(1, 2)),
            jnp.sum(grads * lag_two, axis=(1, 2)),
        ],
        axis=1,
    )
    skip_terms = jnp.sum(upstream * product)
    partials = jnp.concatenate([tap_terms.reshape(-1), skip_terms[None]])
    got_rows, got_partials = with_partner((grads[:, :, 0:2].transpose(0, 2, 1), partials))
    got_rows = got_rows.transpose(0, 2, 1)
    shifted = jnp.concatenate([got_rows[:, 1:], jnp.zeros_like(got_rows[:, :1])], axis=1)
    behind = jnp.concatenate([grads, jnp.where(first, got_rows, shifted)], axis=2)
    stream_grads = (
        weights[:, 0:1, None] * grads
        + weights[:, 1:2, None] * behind[:, :, 1 : half + 1]
        + weights[:, 2:3, None] * behind[:, :, 2 : half + 2]
    )
    factor = 1.0 / math.sqrt(row_count * devices)
    totals = (partials + got_partials) * factor

    payload = jnp.concatenate(
        [gated_output, stream_grads[0], stream_grads[1], stream_grads[2], gradient * factor]
        + [jnp.broadcast_to(totals[None], (devices, totals.shape[0]))],
        axis=1,
    )
    returned = lax.all_to_all(payload, everyone, 0, 0, tiled=True)
    rows_back = (
        returned[:, : 5 * half]
        .reshape(channels, 2, 5, half)
        .transpose(2, 1, 3, 0)
        .reshape(5, row_count, channels)
    )
    per_channel = returned[:, 5 * half :].reshape(channels, 2, -1)[:, 0].T
    tap_total = per_channel[:-1].reshape(3, 3, channels)
    skip_total = per_channel[-1]
    return (rows_back[0], rows_back[1:4], rows_back[4], tap_total, skip_total)


def solution(mesh):
    placed = (
        P(everyone, None),
        P(everyone, None),
        P(everyone, None),
        P(everyone, None),
        P(),
        P(),
        P(everyone, None),
    )
    return jax.shard_map(
        on_device,
        mesh=mesh,
        in_specs=placed,
        out_specs=(
            P(everyone, None),
            P(None, everyone, None),
            P(everyone, None),
            P(),
            P(),
        ),
        check_vma=False,
    )
```

```python
import math

import jax
import jax.numpy as jnp
from jax import lax
from jax.sharding import PartitionSpec as P

exact_mode = lax.Precision.HIGH
everyone = ("outer", "inner")


def passed_along(block, axis, distance):
    devices = range(lax.axis_size(axis))
    route = [(i - distance, i) for i in devices if i - distance in devices]
    return lax.ppermute(block, axis, route)


def with_partner(block):
    devices = lax.axis_size(everyone)
    return lax.ppermute(block, everyone, [(i, i ^ 1) for i in range(devices)])


def unit_angles(counts_table, period):
    return 2.0 * math.pi / period * (counts_table % period).astype(jnp.float32)


def self_position():
    return lax.axis_index("outer") * lax.axis_size("inner") + lax.axis_index("inner")


def in_halves(first, mine, theirs, axis):
    return jnp.where(
        first,
        jnp.concatenate([mine, theirs], axis=axis),
        jnp.concatenate([theirs, mine], axis=axis),
    )


def dot(left, right):
    return jnp.dot(left, right, precision=exact_mode)


def long_convolutions(pieces, row_count):
    members = len(pieces)
    devices = lax.axis_size(everyone)
    half = row_count // 2
    blocks = 2 * devices
    kept = blocks // 2
    length = blocks * row_count
    position = self_position()
    side = position % 2
    first = side == 0
    hidden_zero = position // (4 * devices)

    block_index = jnp.arange(devices, dtype=jnp.int32) + hidden_zero
    coarse = jnp.arange(blocks, dtype=jnp.int32) + hidden_zero
    fine = jnp.arange(row_count, dtype=jnp.int32) + hidden_zero
    coarse_angles = unit_angles(coarse[:, None] * block_index[None, :], blocks)
    coarse_cos = jnp.cos(coarse_angles)
    coarse_sin = jnp.sin(coarse_angles)
    back_angles = unit_angles(block_index[:, None] * coarse[None, :], blocks)
    back_cos = jnp.cos(back_angles)
    back_sin = jnp.sin(back_angles)
    coarse_mine = side * kept + jnp.arange(kept, dtype=jnp.int32)
    twiddle = unit_angles(coarse_mine[:, None] * fine[None, :], length)[None]
    twiddle_cos = jnp.cos(twiddle)
    twiddle_sin = jnp.sin(twiddle)
    fine_angles = unit_angles(fine[:, None] * fine[None, :], row_count)
    fine_cos = jnp.cos(fine_angles)
    fine_sin = jnp.sin(fine_angles)
    (coarse_cos, coarse_sin, back_cos, back_sin, twiddle_cos, twiddle_sin, fine_cos, fine_sin) = (
        lax.optimization_barrier(
            (coarse_cos, coarse_sin, back_cos, back_sin, twiddle_cos, twiddle_sin, fine_cos, fine_sin)
        )
    )

    first_real = jnp.stack([dot(coarse_cos, piece) for piece in pieces])
    first_imag = -jnp.stack([dot(coarse_sin, piece) for piece in pieces])

    def split_coarse(part):
        low, high = part[:, :kept], part[:, kept:]
        return jnp.where(first, low, high), jnp.where(first, high, low)

    keep_real, send_real = split_coarse(first_real)
    keep_imag, send_imag = split_coarse(first_imag)
    got_real, got_imag = with_partner(jnp.stack([send_real, send_imag]))
    full_real = in_halves(first, keep_real, got_real, 2)
    full_imag = in_halves(first, keep_imag, got_imag, 2)

    turned_real = full_real * twiddle_cos + full_imag * twiddle_sin
    turned_imag = full_imag * twiddle_cos - full_real * twiddle_sin

    flat = (members * kept, row_count)
    shape = (members, kept, row_count)
    turned_real = turned_real.reshape(flat)
    turned_imag = turned_imag.reshape(flat)
    spec_real = (dot(turned_real, fine_cos) + dot(turned_imag, fine_sin)).reshape(shape)
    spec_imag = (dot(turned_imag, fine_cos) - dot(turned_real, fine_sin)).reshape(shape)

    filter_real, product_real, upstream_real = (spec_real[0], spec_real[1], spec_real[2])
    filter_imag, product_imag, upstream_imag = (spec_imag[0], spec_imag[1], spec_imag[2])
    causal_real = filter_real * product_real - filter_imag * product_imag
    causal_imag = filter_real * product_imag + filter_imag * product_real
    back_real = filter_real * upstream_real + filter_imag * upstream_imag
    back_imag = filter_real * upstream_imag - filter_imag * upstream_real
    grad_real = product_real * upstream_real + product_imag * upstream_imag
    grad_imag = product_real * upstream_imag - product_imag * upstream_real
    out_real = jnp.stack([causal_real, back_real, grad_real]).reshape(flat)
    out_imag = jnp.stack([causal_imag, back_imag, grad_imag]).reshape(flat)

    inner_real = (dot(out_real, fine_cos) - dot(out_imag, fine_sin)).reshape(shape)
    inner_imag = (dot(out_imag, fine_cos) + dot(out_real, fine_sin)).reshape(shape)
    unturned_real = inner_real * twiddle_cos - inner_imag * twiddle_sin
    unturned_imag = inner_imag * twiddle_cos + inner_real * twiddle_sin

    def split_fine(part):
        low, high = part[:, :, :half], part[:, :, half:]
        return jnp.where(first, low, high), jnp.where(first, high, low)

    mine_real, away_real = split_fine(unturned_real)
    mine_imag, away_imag = split_fine(unturned_imag)
    came_real, came_imag = with_partner(jnp.stack([away_real, away_imag]))
    whole_real = in_halves(first, mine_real, came_real, 1)
    whole_imag = in_halves(first, mine_imag, came_imag, 1)

    scale = 1.0 / length
    return [
        (dot(back_cos, whole_real[m]) - dot(back_sin, whole_imag[m])) * scale
        for m in range(members)
    ]


def on_device(
    query_stream, key_stream, value_stream, filter_taps, skip_gain, short_weights, cotangent
):
    row_count, channels = query_stream.shape
    devices = lax.axis_size(everyone)
    half = row_count // 2
    lane = 128
    position = self_position()
    channel = position // 2

    streams = jnp.stack([query_stream, key_stream, value_stream])
    earlier = passed_along(streams[:, row_count - 2 :, :], everyone, 1)
    ahead = jnp.concatenate([earlier, streams], axis=1)
    mixed = (
        short_weights[:, 0:1] * streams
        + short_weights[:, 1:2] * ahead[:, 1 : row_count + 1]
        + short_weights[:, 2:3] * ahead[:, 0:row_count]
    )

    sent = jnp.stack([query_stream, key_stream, value_stream, filter_taps, cotangent])
    sent = sent.reshape(5, 2, half, channels).transpose(3, 1, 0, 2).reshape(channels, 2, 5 * half)
    halo = jnp.stack([ahead[:, 0:2], ahead[:, half : half + 2]], axis=1)
    halo = halo.transpose(3, 1, 0, 2).reshape(channels, 2, 6)
    halo = jnp.pad(halo, ((0, 0), (0, 0), (0, lane - 6)))
    sent = jnp.concatenate([sent, halo], axis=2).reshape(devices, -1)
    columns = lax.all_to_all(sent, everyone, 0, 0, tiled=True)

    parts = [columns[:, k * half : (k + 1) * half] for k in range(5)]
    own = jnp.stack(parts[:3])
    filter_part, cotangent_part = parts[3], parts[4]
    before = columns[:, 5 * half : 5 * half + 6].reshape(devices, 3, 2).transpose(1, 0, 2)
    padded = jnp.concatenate([before, own], axis=2)
    lag_one = padded[:, :, 1 : half + 1]
    lag_two = padded[:, :, 0:half]
    weights = lax.dynamic_index_in_dim(short_weights, channel, axis=2, keepdims=False)
    gain = lax.dynamic_index_in_dim(skip_gain, channel, axis=0, keepdims=False)
    mixed_part = (
        weights[:, 0:1, None] * own
        + weights[:, 1:2, None] * lag_one
        + weights[:, 2:3, None] * lag_two
    )
    product = mixed_part[1] * mixed_part[2]
    upstream = cotangent_part * mixed_part[0]
    causal, backward_long, gradient = long_convolutions(
        [filter_part, product, upstream], row_count
    )
    summed_part = causal + gain * product
    backward_part = backward_long + gain * upstream
    grads_part = jnp.stack(
        [cotangent_part * summed_part, backward_part * mixed_part[2], backward_part * mixed_part[1]]
    )
    tap_terms = jnp.stack(
        [
            jnp.sum(grads_part * own, axis=(1, 2)),
            jnp.sum(grads_part * lag_one, axis=(1, 2)),
            jnp.sum(grads_part * lag_two, axis=(1, 2)),
        ],
        axis=1,
    )
    skip_terms = jnp.sum(upstream * product)
    partials = jnp.concatenate([tap_terms.reshape(-1), skip_terms[None]])
    factor = 1.0 / math.sqrt(row_count * devices)
    totals = (partials + with_partner(partials)) * factor
    totals = jnp.pad(
        jnp.broadcast_to(totals[None], (devices, totals.shape[0])),
        ((0, 0), (0, lane - totals.shape[0])),
    )

    payload = jnp.concatenate([summed_part, backward_part, gradient * factor, totals], axis=1)
    returned = lax.all_to_all(payload, everyone, 0, 0, tiled=True)
    summed, backward, filter_grad = (
        returned[:, : 3 * half]
        .reshape(channels, 2, 3, half)
        .transpose(2, 1, 3, 0)
        .reshape(3, row_count, channels)
    )
    per_channel = returned[:, 3 * half : 3 * half + 10].reshape(channels, 2, 10)[:, 0].T
    tap_total = per_channel[:-1].reshape(3, 3, channels)
    skip_total = per_channel[-1]

    gated_output = mixed[0] * summed
    grads = jnp.stack([cotangent * summed, backward * mixed[2], backward * mixed[1]])
    later = passed_along(grads[:, 0:2, :], everyone, -1)
    behind = jnp.concatenate([grads, later], axis=1)
    stream_grads = (
        short_weights[:, 0:1] * grads
        + short_weights[:, 1:2] * behind[:, 1 : row_count + 1]
        + short_weights[:, 2:3] * behind[:, 2 : row_count + 2]
    )
    return (gated_output, stream_grads, filter_grad, tap_total, skip_total)


def solution(mesh):
    placed = (
        P(everyone, None),
        P(everyone, None),
        P(everyone, None),
        P(everyone, None),
        P(),
        P(),
        P(everyone, None),
    )
    return jax.shard_map(
        on_device,
        mesh=mesh,
        in_specs=placed,
        out_specs=(
            P(everyone, None),
            P(None, everyone, None),
            P(everyone, None),
            P(),
            P(),
        ),
        check_vma=False,
    )
```

```python
import math

import jax
import jax.numpy as jnp
from jax import lax
from jax.sharding import PartitionSpec as P

exact_mode = lax.Precision.HIGH
everyone = ("outer", "inner")


def passed_along(block, axis, distance):
    devices = range(lax.axis_size(axis))
    route = [(i - distance, i) for i in devices if i - distance in devices]
    return lax.ppermute(block, axis, route)


def with_partner(block):
    devices = lax.axis_size(everyone)
    return lax.ppermute(block, everyone, [(i, i ^ 1) for i in range(devices)])


def unit_angles(counts_table, period):
    return 2.0 * math.pi / period * (counts_table % period).astype(jnp.float32)


def self_position():
    return lax.axis_index("outer") * lax.axis_size("inner") + lax.axis_index("inner")


def in_halves(first, mine, theirs, axis):
    return jnp.where(
        first,
        jnp.concatenate([mine, theirs], axis=axis),
        jnp.concatenate([theirs, mine], axis=axis),
    )


def dot(left, right):
    return jnp.dot(left, right, precision=exact_mode)


def long_convolutions(pieces, row_count):
    members = len(pieces)
    devices = lax.axis_size(everyone)
    half = row_count // 2
    blocks = 2 * devices
    kept = blocks // 2
    length = blocks * row_count
    position = self_position()
    side = position % 2
    first = side == 0
    hidden_zero = position // (4 * devices)

    block_index = jnp.arange(devices, dtype=jnp.int32) + hidden_zero
    coarse = jnp.arange(blocks, dtype=jnp.int32) + hidden_zero
    fine = jnp.arange(row_count, dtype=jnp.int32) + hidden_zero
    coarse_angles = unit_angles(coarse[:, None] * block_index[None, :], blocks)
    coarse_cos = jnp.cos(coarse_angles)
    coarse_sin = jnp.sin(coarse_angles)
    back_angles = unit_angles(block_index[:, None] * coarse[None, :], blocks)
    back_cos = jnp.cos(back_angles)
    back_sin = jnp.sin(back_angles)
    coarse_mine = side * kept + jnp.arange(kept, dtype=jnp.int32)
    twiddle = unit_angles(coarse_mine[:, None] * fine[None, :], length)[None]
    twiddle_cos = jnp.cos(twiddle)
    twiddle_sin = jnp.sin(twiddle)
    fine_angles = unit_angles(fine[:, None] * fine[None, :], row_count)
    fine_cos = jnp.cos(fine_angles)
    fine_sin = jnp.sin(fine_angles)
    (coarse_cos, coarse_sin, back_cos, back_sin, twiddle_cos, twiddle_sin, fine_cos, fine_sin) = (
        lax.optimization_barrier(
            (coarse_cos, coarse_sin, back_cos, back_sin, twiddle_cos, twiddle_sin, fine_cos, fine_sin)
        )
    )

    first_real = jnp.stack([dot(coarse_cos, piece) for piece in pieces])
    first_imag = -jnp.stack([dot(coarse_sin, piece) for piece in pieces])

    def split_coarse(part):
        low, high = part[:, :kept], part[:, kept:]
        return jnp.where(first, low, high), jnp.where(first, high, low)

    keep_real, send_real = split_coarse(first_real)
    keep_imag, send_imag = split_coarse(first_imag)
    got_real, got_imag = with_partner(jnp.stack([send_real, send_imag]))
    full_real = in_halves(first, keep_real, got_real, 2)
    full_imag = in_halves(first, keep_imag, got_imag, 2)

    turned_real = full_real * twiddle_cos + full_imag * twiddle_sin
    turned_imag = full_imag * twiddle_cos - full_real * twiddle_sin

    flat = (members * kept, row_count)
    shape = (members, kept, row_count)
    turned_real = turned_real.reshape(flat)
    turned_imag = turned_imag.reshape(flat)
    spec_real = (dot(turned_real, fine_cos) + dot(turned_imag, fine_sin)).reshape(shape)
    spec_imag = (dot(turned_imag, fine_cos) - dot(turned_real, fine_sin)).reshape(shape)

    filter_real, product_real, upstream_real = (spec_real[0], spec_real[1], spec_real[2])
    filter_imag, product_imag, upstream_imag = (spec_imag[0], spec_imag[1], spec_imag[2])
    causal_real = filter_real * product_real - filter_imag * product_imag
    causal_imag = filter_real * product_imag + filter_imag * product_real
    back_real = filter_real * upstream_real + filter_imag * upstream_imag
    back_imag = filter_real * upstream_imag - filter_imag * upstream_real
    grad_real = product_real * upstream_real + product_imag * upstream_imag
    grad_imag = product_real * upstream_imag - product_imag * upstream_real
    out_real = jnp.stack([causal_real, back_real, grad_real]).reshape(flat)
    out_imag = jnp.stack([causal_imag, back_imag, grad_imag]).reshape(flat)

    inner_real = (dot(out_real, fine_cos) - dot(out_imag, fine_sin)).reshape(shape)
    inner_imag = (dot(out_imag, fine_cos) + dot(out_real, fine_sin)).reshape(shape)
    unturned_real = inner_real * twiddle_cos - inner_imag * twiddle_sin
    unturned_imag = inner_imag * twiddle_cos + inner_real * twiddle_sin

    def split_fine(part):
        low, high = part[:, :, :half], part[:, :, half:]
        return jnp.where(first, low, high), jnp.where(first, high, low)

    mine_real, away_real = split_fine(unturned_real)
    mine_imag, away_imag = split_fine(unturned_imag)
    came_real, came_imag = with_partner(jnp.stack([away_real, away_imag]))
    whole_real = in_halves(first, mine_real, came_real, 1)
    whole_imag = in_halves(first, mine_imag, came_imag, 1)

    scale = 1.0 / length
    return [
        (dot(back_cos, whole_real[m]) - dot(back_sin, whole_imag[m])) * scale
        for m in range(members)
    ]


def on_device(
    query_stream, key_stream, value_stream, filter_taps, skip_gain, short_weights, cotangent
):
    row_count, channels = query_stream.shape
    devices = lax.axis_size(everyone)
    half = row_count // 2
    lane = 128
    position = self_position()
    channel = position // 2

    streams = jnp.stack([query_stream, key_stream, value_stream])
    earlier = passed_along(streams[:, row_count - 2 :, :], everyone, 1)
    ahead = jnp.concatenate([earlier, streams], axis=1)
    mixed = (
        short_weights[:, 0:1] * streams
        + short_weights[:, 1:2] * ahead[:, 1 : row_count + 1]
        + short_weights[:, 2:3] * ahead[:, 0:row_count]
    )

    def by_channel(block):
        return block.reshape(2, half, channels).transpose(2, 0, 1)

    halo = jnp.stack([ahead[:, 0:2], ahead[:, half : half + 2]], axis=1)
    halo = halo.transpose(3, 1, 0, 2).reshape(channels, 2, 6)
    halo = jnp.pad(halo, ((0, 0), (0, 0), (0, lane - 6)))
    sent = jnp.concatenate(
        [by_channel(b) for b in (query_stream, key_stream, value_stream, filter_taps, cotangent)]
        + [halo],
        axis=2,
    ).reshape(devices, -1)
    columns = lax.all_to_all(sent, everyone, 0, 0, tiled=True)

    parts = [columns[:, k * half : (k + 1) * half] for k in range(5)]
    filter_part, cotangent_part = parts[3], parts[4]
    before = columns[:, 5 * half : 5 * half + 6]
    weights = lax.dynamic_index_in_dim(short_weights, channel, axis=2, keepdims=False)
    gain = lax.dynamic_index_in_dim(skip_gain, channel, axis=0, keepdims=False)
    own, lag_one, lag_two, mixed_part = [], [], [], []
    for s in range(3):
        padded = jnp.concatenate([before[:, 2 * s : 2 * s + 2], parts[s]], axis=1)
        own.append(parts[s])
        lag_one.append(padded[:, 1 : half + 1])
        lag_two.append(padded[:, 0:half])
        mixed_part.append(
            weights[s, 0] * own[s] + weights[s, 1] * lag_one[s] + weights[s, 2] * lag_two[s]
        )
    product = mixed_part[1] * mixed_part[2]
    upstream = cotangent_part * mixed_part[0]
    causal, backward_long, gradient = long_convolutions(
        [filter_part, product, upstream], row_count
    )
    summed_part = causal + gain * product
    backward_part = backward_long + gain * upstream
    grads_part = [
        cotangent_part * summed_part,
        backward_part * mixed_part[2],
        backward_part * mixed_part[1],
    ]
    tap_terms = jnp.stack(
        [
            jnp.stack([jnp.sum(grads_part[s] * lagged[s]) for lagged in (own, lag_one, lag_two)])
            for s in range(3)
        ]
    )
    skip_terms = jnp.sum(upstream * product)
    partials = jnp.concatenate([tap_terms.reshape(-1), skip_terms[None]])
    factor = 1.0 / math.sqrt(row_count * devices)
    totals = (partials + with_partner(partials)) * factor
    totals = jnp.pad(
        jnp.broadcast_to(totals[None], (devices, totals.shape[0])),
        ((0, 0), (0, lane - totals.shape[0])),
    )

    payload = jnp.concatenate([summed_part, backward_part, gradient * factor, totals], axis=1)
    returned = lax.all_to_all(payload, everyone, 0, 0, tiled=True)
    summed, backward, filter_grad = (
        returned[:, : 3 * half]
        .reshape(channels, 2, 3, half)
        .transpose(2, 1, 3, 0)
        .reshape(3, row_count, channels)
    )
    per_channel = returned[:, 3 * half : 3 * half + 10].reshape(channels, 2, 10)[:, 0].T
    tap_total = per_channel[:-1].reshape(3, 3, channels)
    skip_total = per_channel[-1]

    gated_output = mixed[0] * summed
    grads = jnp.stack([cotangent * summed, backward * mixed[2], backward * mixed[1]])
    later = passed_along(grads[:, 0:2, :], everyone, -1)
    behind = jnp.concatenate([grads, later], axis=1)
    stream_grads = (
        short_weights[:, 0:1] * grads
        + short_weights[:, 1:2] * behind[:, 1 : row_count + 1]
        + short_weights[:, 2:3] * behind[:, 2 : row_count + 2]
    )
    return (gated_output, stream_grads, filter_grad, tap_total, skip_total)


def solution(mesh):
    placed = (
        P(everyone, None),
        P(everyone, None),
        P(everyone, None),
        P(everyone, None),
        P(),
        P(),
        P(everyone, None),
    )
    return jax.shard_map(
        on_device,
        mesh=mesh,
        in_specs=placed,
        out_specs=(
            P(everyone, None),
            P(None, everyone, None),
            P(everyone, None),
            P(),
            P(),
        ),
        check_vma=False,
    )
```

```python
import math

import jax
import jax.numpy as jnp
from jax import lax
from jax.sharding import PartitionSpec as P

exact_mode = lax.Precision.HIGH
everyone = ("outer", "inner")


def passed_along(block, axis, distance):
    devices = range(lax.axis_size(axis))
    route = [(i - distance, i) for i in devices if i - distance in devices]
    return lax.ppermute(block, axis, route)


def with_partner(block):
    devices = lax.axis_size(everyone)
    return lax.ppermute(block, everyone, [(i, i ^ 1) for i in range(devices)])


def unit_angles(counts_table, period):
    return 2.0 * math.pi / period * (counts_table % period).astype(jnp.float32)


def self_position():
    return lax.axis_index("outer") * lax.axis_size("inner") + lax.axis_index("inner")


def in_halves(first, mine, theirs, axis):
    return jnp.where(
        first,
        jnp.concatenate([mine, theirs], axis=axis),
        jnp.concatenate([theirs, mine], axis=axis),
    )


def dot(left, right):
    return jnp.dot(left, right, precision=exact_mode)


def long_convolutions(pieces, row_count):
    members = len(pieces)
    devices = lax.axis_size(everyone)
    half = row_count // 2
    blocks = 2 * devices
    kept = blocks // 2
    length = blocks * row_count
    position = self_position()
    side = position % 2
    first = side == 0
    hidden_zero = position // (4 * devices)

    block_index = jnp.arange(devices, dtype=jnp.int32) + hidden_zero
    coarse = jnp.arange(blocks, dtype=jnp.int32) + hidden_zero
    fine = jnp.arange(row_count, dtype=jnp.int32) + hidden_zero
    coarse_angles = unit_angles(coarse[:, None] * block_index[None, :], blocks)
    coarse_cos = jnp.cos(coarse_angles)
    coarse_sin = jnp.sin(coarse_angles)
    back_angles = unit_angles(block_index[:, None] * coarse[None, :], blocks)
    back_cos = jnp.cos(back_angles)
    back_sin = jnp.sin(back_angles)
    coarse_mine = side * kept + jnp.arange(kept, dtype=jnp.int32)
    twiddle = unit_angles(coarse_mine[:, None] * fine[None, :], length)[None]
    twiddle_cos = jnp.cos(twiddle)
    twiddle_sin = jnp.sin(twiddle)
    fine_angles = unit_angles(fine[:, None] * fine[None, :], row_count)
    fine_cos = jnp.cos(fine_angles)
    fine_sin = jnp.sin(fine_angles)
    (coarse_cos, coarse_sin, back_cos, back_sin, twiddle_cos, twiddle_sin, fine_cos, fine_sin) = (
        lax.optimization_barrier(
            (coarse_cos, coarse_sin, back_cos, back_sin, twiddle_cos, twiddle_sin, fine_cos, fine_sin)
        )
    )

    first_real = jnp.stack([dot(coarse_cos, piece) for piece in pieces])
    first_imag = -jnp.stack([dot(coarse_sin, piece) for piece in pieces])

    def split_coarse(part):
        low, high = part[:, :kept], part[:, kept:]
        return jnp.where(first, low, high), jnp.where(first, high, low)

    keep_real, send_real = split_coarse(first_real)
    keep_imag, send_imag = split_coarse(first_imag)
    got_real, got_imag = with_partner(jnp.stack([send_real, send_imag]))
    full_real = in_halves(first, keep_real, got_real, 2)
    full_imag = in_halves(first, keep_imag, got_imag, 2)

    turned_real = full_real * twiddle_cos + full_imag * twiddle_sin
    turned_imag = full_imag * twiddle_cos - full_real * twiddle_sin

    flat = (members * kept, row_count)
    shape = (members, kept, row_count)
    turned_real = turned_real.reshape(flat)
    turned_imag = turned_imag.reshape(flat)
    spec_real = (dot(turned_real, fine_cos) + dot(turned_imag, fine_sin)).reshape(shape)
    spec_imag = (dot(turned_imag, fine_cos) - dot(turned_real, fine_sin)).reshape(shape)

    filter_real, product_real, upstream_real = (spec_real[0], spec_real[1], spec_real[2])
    filter_imag, product_imag, upstream_imag = (spec_imag[0], spec_imag[1], spec_imag[2])
    causal_real = filter_real * product_real - filter_imag * product_imag
    causal_imag = filter_real * product_imag + filter_imag * product_real
    back_real = filter_real * upstream_real + filter_imag * upstream_imag
    back_imag = filter_real * upstream_imag - filter_imag * upstream_real
    grad_real = product_real * upstream_real + product_imag * upstream_imag
    grad_imag = product_real * upstream_imag - product_imag * upstream_real
    out_real = jnp.stack([causal_real, back_real, grad_real]).reshape(flat)
    out_imag = jnp.stack([causal_imag, back_imag, grad_imag]).reshape(flat)

    inner_real = (dot(out_real, fine_cos) - dot(out_imag, fine_sin)).reshape(shape)
    inner_imag = (dot(out_imag, fine_cos) + dot(out_real, fine_sin)).reshape(shape)
    unturned_real = inner_real * twiddle_cos - inner_imag * twiddle_sin
    unturned_imag = inner_imag * twiddle_cos + inner_real * twiddle_sin

    def split_fine(part):
        low, high = part[:, :, :half], part[:, :, half:]
        return jnp.where(first, low, high), jnp.where(first, high, low)

    mine_real, away_real = split_fine(unturned_real)
    mine_imag, away_imag = split_fine(unturned_imag)
    came_real, came_imag = with_partner(jnp.stack([away_real, away_imag]))
    whole_real = in_halves(first, mine_real, came_real, 1)
    whole_imag = in_halves(first, mine_imag, came_imag, 1)

    scale = 1.0 / length
    return [
        (dot(back_cos, whole_real[m]) - dot(back_sin, whole_imag[m])) * scale
        for m in range(members)
    ]


def on_device(
    query_stream, key_stream, value_stream, filter_taps, skip_gain, short_weights, cotangent
):
    row_count, channels = query_stream.shape
    devices = lax.axis_size(everyone)
    half = row_count // 2
    lane = 128
    position = self_position()
    channel = position // 2

    streams = jnp.stack([query_stream, key_stream, value_stream])
    earlier = passed_along(streams[:, row_count - 2 :, :], everyone, 1)
    ahead = jnp.concatenate([earlier, streams], axis=1)
    mixed = (
        short_weights[:, 0:1] * streams
        + short_weights[:, 1:2] * ahead[:, 1 : row_count + 1]
        + short_weights[:, 2:3] * ahead[:, 0:row_count]
    )

    def by_channel(block):
        return block.reshape(2, half, channels).transpose(2, 0, 1)

    halo = jnp.stack([ahead[:, 0:2], ahead[:, half : half + 2]], axis=1)
    halo = halo.transpose(3, 1, 0, 2).reshape(channels, 2, 6)
    halo = jnp.pad(halo, ((0, 0), (0, 0), (0, lane - 6)))
    sent = jnp.concatenate(
        [by_channel(b) for b in (query_stream, key_stream, value_stream, filter_taps, cotangent)]
        + [halo],
        axis=2,
    ).reshape(devices, -1)
    columns = lax.all_to_all(sent, everyone, 0, 0, tiled=True)

    parts = [columns[:, k * half : (k + 1) * half] for k in range(5)]
    own = jnp.stack(parts[:3])
    filter_part, cotangent_part = parts[3], parts[4]
    before = columns[:, 5 * half : 5 * half + 6].reshape(devices, 3, 2).transpose(1, 0, 2)
    padded = jnp.concatenate([before, own], axis=2)
    lag_one = padded[:, :, 1 : half + 1]
    lag_two = padded[:, :, 0:half]
    weights = lax.dynamic_index_in_dim(short_weights, channel, axis=2, keepdims=False)
    gain = lax.dynamic_index_in_dim(skip_gain, channel, axis=0, keepdims=False)
    mixed_part = (
        weights[:, 0:1, None] * own
        + weights[:, 1:2, None] * lag_one
        + weights[:, 2:3, None] * lag_two
    )
    product = mixed_part[1] * mixed_part[2]
    upstream = cotangent_part * mixed_part[0]
    causal, backward_long, gradient = long_convolutions(
        [filter_part, product, upstream], row_count
    )
    summed_part = causal + gain * product
    backward_part = backward_long + gain * upstream
    grads_part = jnp.stack(
        [cotangent_part * summed_part, backward_part * mixed_part[2], backward_part * mixed_part[1]]
    )
    tap_terms = jnp.stack(
        [
            jnp.sum(grads_part * own, axis=(1, 2)),
            jnp.sum(grads_part * lag_one, axis=(1, 2)),
            jnp.sum(grads_part * lag_two, axis=(1, 2)),
        ],
        axis=1,
    )
    skip_terms = jnp.sum(upstream * product)
    partials = jnp.concatenate([tap_terms.reshape(-1), skip_terms[None]])
    factor = 1.0 / math.sqrt(row_count * devices)
    totals = (partials + with_partner(partials)) * factor
    totals = jnp.pad(
        jnp.broadcast_to(totals[None], (devices, totals.shape[0])),
        ((0, 0), (0, lane - totals.shape[0])),
    )

    payload = jnp.concatenate([summed_part, backward_part, gradient * factor, totals], axis=1)
    returned = lax.all_to_all(payload, everyone, 0, 0, tiled=True)
    summed, backward, filter_grad = (
        returned[:, : 3 * half]
        .reshape(channels, 2, 3, half)
        .transpose(2, 1, 3, 0)
        .reshape(3, row_count, channels)
    )
    per_channel = returned[:, 3 * half : 3 * half + 10].reshape(channels, 2, 10)[:, 0].T
    tap_total = per_channel[:-1].reshape(3, 3, channels)
    skip_total = per_channel[-1]

    gated_output = mixed[0] * summed
    grads = jnp.stack([cotangent * summed, backward * mixed[2], backward * mixed[1]])
    later = passed_along(grads[:, 0:2, :], everyone, -1)
    behind = jnp.concatenate([grads, later], axis=1)
    stream_grads = (
        short_weights[:, 0:1] * grads
        + short_weights[:, 1:2] * behind[:, 1 : row_count + 1]
        + short_weights[:, 2:3] * behind[:, 2 : row_count + 2]
    )
    return (gated_output, stream_grads, filter_grad, tap_total, skip_total)


def solution(mesh):
    placed = (
        P(everyone, None),
        P(everyone, None),
        P(everyone, None),
        P(everyone, None),
        P(),
        P(),
        P(everyone, None),
    )
    return jax.shard_map(
        on_device,
        mesh=mesh,
        in_specs=placed,
        out_specs=(
            P(everyone, None),
            P(None, everyone, None),
            P(everyone, None),
            P(),
            P(),
        ),
        check_vma=False,
    )
```

```python
import math

import jax
import jax.numpy as jnp
from jax import lax
from jax.sharding import PartitionSpec as P

exact_mode = lax.Precision.HIGH
everyone = ("outer", "inner")


def passed_along(block, axis, distance):
    devices = range(lax.axis_size(axis))
    route = [(i - distance, i) for i in devices if i - distance in devices]
    return lax.ppermute(block, axis, route)


def with_partner(block):
    devices = lax.axis_size(everyone)
    return lax.ppermute(block, everyone, [(i, i ^ 1) for i in range(devices)])


def unit_angles(counts_table, period):
    return 2.0 * math.pi / period * (counts_table % period).astype(jnp.float32)


def self_position():
    return lax.axis_index("outer") * lax.axis_size("inner") + lax.axis_index("inner")


def in_halves(first, mine, theirs, axis):
    return jnp.where(
        first,
        jnp.concatenate([mine, theirs], axis=axis),
        jnp.concatenate([theirs, mine], axis=axis),
    )


def dot(left, right):
    return jnp.dot(left, right, precision=exact_mode)


def long_convolutions(pieces, row_count):
    members = len(pieces)
    devices = lax.axis_size(everyone)
    half = row_count // 2
    blocks = 2 * devices
    kept = blocks // 2
    length = blocks * row_count
    position = self_position()
    side = position % 2
    first = side == 0
    hidden_zero = position // (4 * devices)

    block_index = jnp.arange(devices, dtype=jnp.int32) + hidden_zero
    coarse = jnp.arange(blocks, dtype=jnp.int32) + hidden_zero
    fine = jnp.arange(row_count, dtype=jnp.int32) + hidden_zero
    coarse_angles = unit_angles(coarse[:, None] * block_index[None, :], blocks)
    coarse_cos = jnp.cos(coarse_angles)
    coarse_sin = jnp.sin(coarse_angles)
    back_angles = unit_angles(block_index[:, None] * coarse[None, :], blocks)
    back_cos = jnp.cos(back_angles)
    back_sin = jnp.sin(back_angles)
    coarse_mine = side * kept + jnp.arange(kept, dtype=jnp.int32)
    twiddle = unit_angles(coarse_mine[:, None] * fine[None, :], length)[None]
    twiddle_cos = jnp.cos(twiddle)
    twiddle_sin = jnp.sin(twiddle)
    fine_angles = unit_angles(fine[:, None] * fine[None, :], row_count)
    fine_cos = jnp.cos(fine_angles)
    fine_sin = jnp.sin(fine_angles)
    (coarse_cos, coarse_sin, back_cos, back_sin, twiddle_cos, twiddle_sin, fine_cos, fine_sin) = (
        lax.optimization_barrier(
            (coarse_cos, coarse_sin, back_cos, back_sin, twiddle_cos, twiddle_sin, fine_cos, fine_sin)
        )
    )

    first_real = jnp.stack([dot(coarse_cos, piece) for piece in pieces])
    first_imag = -jnp.stack([dot(coarse_sin, piece) for piece in pieces])

    def split_coarse(part):
        low, high = part[:, :kept], part[:, kept:]
        return jnp.where(first, low, high), jnp.where(first, high, low)

    keep_real, send_real = split_coarse(first_real)
    keep_imag, send_imag = split_coarse(first_imag)
    got_real, got_imag = with_partner(jnp.stack([send_real, send_imag]))
    full_real = in_halves(first, keep_real, got_real, 2)
    full_imag = in_halves(first, keep_imag, got_imag, 2)

    turned_real = full_real * twiddle_cos + full_imag * twiddle_sin
    turned_imag = full_imag * twiddle_cos - full_real * twiddle_sin

    flat = (members * kept, row_count)
    shape = (members, kept, row_count)
    turned_real = turned_real.reshape(flat)
    turned_imag = turned_imag.reshape(flat)
    spec_real = (dot(turned_real, fine_cos) + dot(turned_imag, fine_sin)).reshape(shape)
    spec_imag = (dot(turned_imag, fine_cos) - dot(turned_real, fine_sin)).reshape(shape)

    filter_real, product_real, upstream_real = (spec_real[0], spec_real[1], spec_real[2])
    filter_imag, product_imag, upstream_imag = (spec_imag[0], spec_imag[1], spec_imag[2])
    causal_real = filter_real * product_real - filter_imag * product_imag
    causal_imag = filter_real * product_imag + filter_imag * product_real
    back_real = filter_real * upstream_real + filter_imag * upstream_imag
    back_imag = filter_real * upstream_imag - filter_imag * upstream_real
    grad_real = product_real * upstream_real + product_imag * upstream_imag
    grad_imag = product_real * upstream_imag - product_imag * upstream_real
    out_real = jnp.stack([causal_real, back_real, grad_real]).reshape(flat)
    out_imag = jnp.stack([causal_imag, back_imag, grad_imag]).reshape(flat)

    inner_real = (dot(out_real, fine_cos) - dot(out_imag, fine_sin)).reshape(shape)
    inner_imag = (dot(out_imag, fine_cos) + dot(out_real, fine_sin)).reshape(shape)
    unturned_real = inner_real * twiddle_cos - inner_imag * twiddle_sin
    unturned_imag = inner_imag * twiddle_cos + inner_real * twiddle_sin

    def split_fine(part):
        low, high = part[:, :, :half], part[:, :, half:]
        return jnp.where(first, low, high), jnp.where(first, high, low)

    mine_real, away_real = split_fine(unturned_real)
    mine_imag, away_imag = split_fine(unturned_imag)
    came_real, came_imag = with_partner(jnp.stack([away_real, away_imag]))
    whole_real = in_halves(first, mine_real, came_real, 1)
    whole_imag = in_halves(first, mine_imag, came_imag, 1)

    scale = 1.0 / length
    return [
        (dot(back_cos, whole_real[m]) - dot(back_sin, whole_imag[m])) * scale
        for m in range(members)
    ]


def on_device(
    query_stream, key_stream, value_stream, filter_taps, skip_gain, short_weights, cotangent
):
    row_count, channels = query_stream.shape
    devices = lax.axis_size(everyone)
    half = row_count // 2
    lane = 128
    position = self_position()
    channel = position // 2

    streams = jnp.stack([query_stream, key_stream, value_stream])
    earlier = passed_along(streams[:, row_count - 2 :, :], everyone, 1)
    ahead = jnp.concatenate([earlier, streams], axis=1)
    mixed = (
        short_weights[:, 0:1] * streams
        + short_weights[:, 1:2] * ahead[:, 1 : row_count + 1]
        + short_weights[:, 2:3] * ahead[:, 0:row_count]
    )

    def by_channel(block):
        return block.reshape(2, half, channels).transpose(2, 0, 1)

    halo = jnp.stack([ahead[:, 0:2], ahead[:, half : half + 2]], axis=1)
    halo = halo.transpose(3, 1, 0, 2).reshape(channels, 2, 6)
    halo = jnp.pad(halo, ((0, 0), (0, 0), (0, lane - 6)))
    sent = jnp.concatenate(
        [by_channel(b) for b in (query_stream, key_stream, value_stream, filter_taps, cotangent)]
        + [halo],
        axis=2,
    ).reshape(devices, -1)
    columns = lax.all_to_all(sent, everyone, 0, 0, tiled=True)

    parts = [columns[:, k * half : (k + 1) * half] for k in range(5)]
    own = jnp.stack(parts[:3])
    filter_part, cotangent_part = parts[3], parts[4]
    before = columns[:, 5 * half : 5 * half + 6].reshape(devices, 3, 2).transpose(1, 0, 2)
    padded = jnp.concatenate([before, own], axis=2)
    lag_one = padded[:, :, 1 : half + 1]
    lag_two = padded[:, :, 0:half]
    weights = lax.dynamic_index_in_dim(short_weights, channel, axis=2, keepdims=False)
    gain = lax.dynamic_index_in_dim(skip_gain, channel, axis=0, keepdims=False)
    mixed_part = (
        weights[:, 0:1, None] * own
        + weights[:, 1:2, None] * lag_one
        + weights[:, 2:3, None] * lag_two
    )
    product = mixed_part[1] * mixed_part[2]
    upstream = cotangent_part * mixed_part[0]
    causal, backward_long, gradient = long_convolutions(
        [filter_part, product, upstream], row_count
    )
    summed_part = causal + gain * product
    backward_part = backward_long + gain * upstream
    grads_part = jnp.stack(
        [cotangent_part * summed_part, backward_part * mixed_part[2], backward_part * mixed_part[1]]
    )
    tap_terms = jnp.stack(
        [
            jnp.sum(grads_part * own, axis=(1, 2)),
            jnp.sum(grads_part * lag_one, axis=(1, 2)),
            jnp.sum(grads_part * lag_two, axis=(1, 2)),
        ],
        axis=1,
    )
    skip_terms = jnp.sum(upstream * product)
    partials = jnp.concatenate([tap_terms.reshape(-1), skip_terms[None]])
    factor = 1.0 / math.sqrt(row_count * devices)
    totals = (partials + with_partner(partials)) * factor
    following = grads_part[:, :, 0:2]
    following = jnp.concatenate([following[:, 1:], jnp.zeros_like(following[:, :1])], axis=1)
    extra = jnp.concatenate(
        [
            jnp.broadcast_to(totals[None], (devices, totals.shape[0])),
            following.transpose(1, 0, 2).reshape(devices, 6),
        ],
        axis=1,
    )
    extra = jnp.pad(extra, ((0, 0), (0, lane - extra.shape[1])))

    payload = jnp.concatenate([summed_part, backward_part, gradient * factor, extra], axis=1)
    returned = lax.all_to_all(payload, everyone, 0, 0, tiled=True)
    summed, backward, filter_grad = (
        returned[:, : 3 * half]
        .reshape(channels, 2, 3, half)
        .transpose(2, 1, 3, 0)
        .reshape(3, row_count, channels)
    )
    extra = returned[:, 3 * half : 3 * half + 16].reshape(channels, 2, 16)[:, 0]
    per_channel = extra[:, :10].T
    later = extra[:, 10:16].reshape(channels, 3, 2).transpose(1, 2, 0)
    tap_total = per_channel[:-1].reshape(3, 3, channels)
    skip_total = per_channel[-1]

    gated_output = mixed[0] * summed
    grads = jnp.stack([cotangent * summed, backward * mixed[2], backward * mixed[1]])
    behind = jnp.concatenate([grads, later], axis=1)
    stream_grads = (
        short_weights[:, 0:1] * grads
        + short_weights[:, 1:2] * behind[:, 1 : row_count + 1]
        + short_weights[:, 2:3] * behind[:, 2 : row_count + 2]
    )
    return (gated_output, stream_grads, filter_grad, tap_total, skip_total)


def solution(mesh):
    placed = (
        P(everyone, None),
        P(everyone, None),
        P(everyone, None),
        P(everyone, None),
        P(),
        P(),
        P(everyone, None),
    )
    return jax.shard_map(
        on_device,
        mesh=mesh,
        in_specs=placed,
        out_specs=(
            P(everyone, None),
            P(None, everyone, None),
            P(everyone, None),
            P(),
            P(),
        ),
        check_vma=False,
    )
```

```python
import math

import jax
import jax.numpy as jnp
from jax import lax
from jax.sharding import PartitionSpec as P

exact_mode = lax.Precision.HIGH
everyone = ("outer", "inner")


def passed_along(block, axis, distance):
    devices = range(lax.axis_size(axis))
    route = [(i - distance, i) for i in devices if i - distance in devices]
    return lax.ppermute(block, axis, route)


def with_partner(block):
    devices = lax.axis_size(everyone)
    return lax.ppermute(block, everyone, [(i, i ^ 1) for i in range(devices)])


def unit_angles(counts_table, period):
    return 2.0 * math.pi / period * (counts_table % period).astype(jnp.float32)


def self_position():
    return lax.axis_index("outer") * lax.axis_size("inner") + lax.axis_index("inner")


def in_halves(first, mine, theirs, axis):
    return jnp.where(
        first,
        jnp.concatenate([mine, theirs], axis=axis),
        jnp.concatenate([theirs, mine], axis=axis),
    )


def dot(left, right):
    return jnp.dot(left, right, precision=exact_mode)


def long_convolutions(pieces, row_count):
    members = len(pieces)
    devices = lax.axis_size(everyone)
    half = row_count // 2
    blocks = 2 * devices
    kept = blocks // 2
    length = blocks * row_count
    position = self_position()
    side = position % 2
    first = side == 0
    hidden_zero = position // (4 * devices)

    block_index = jnp.arange(devices, dtype=jnp.int32) + hidden_zero
    coarse = jnp.arange(blocks, dtype=jnp.int32) + hidden_zero
    fine = jnp.arange(row_count, dtype=jnp.int32) + hidden_zero
    coarse_angles = unit_angles(coarse[:, None] * block_index[None, :], blocks)
    coarse_cos = jnp.cos(coarse_angles)
    coarse_sin = jnp.sin(coarse_angles)
    back_angles = unit_angles(block_index[:, None] * coarse[None, :], blocks)
    back_cos = jnp.cos(back_angles)
    back_sin = jnp.sin(back_angles)
    coarse_mine = side * kept + jnp.arange(kept, dtype=jnp.int32)
    twiddle = unit_angles(coarse_mine[:, None] * fine[None, :], length)[None]
    twiddle_cos = jnp.cos(twiddle)
    twiddle_sin = jnp.sin(twiddle)
    fine_angles = unit_angles(fine[:, None] * fine[None, :], row_count)
    fine_cos = jnp.cos(fine_angles)
    fine_sin = jnp.sin(fine_angles)
    fine_diff = fine_cos - fine_sin
    fine_sum = fine_cos + fine_sin
    tables = (coarse_cos, coarse_sin, back_cos, back_sin, twiddle_cos, twiddle_sin)
    tables += (fine_cos, fine_sin, fine_diff, fine_sum)
    (coarse_cos, coarse_sin, back_cos, back_sin, twiddle_cos, twiddle_sin) = (
        tables := lax.optimization_barrier(tables)
    )[:6]
    fine_cos, fine_sin, fine_diff, fine_sum = tables[6:]

    first_real = jnp.stack([dot(coarse_cos, piece) for piece in pieces])
    first_imag = -jnp.stack([dot(coarse_sin, piece) for piece in pieces])

    def split_coarse(part):
        low, high = part[:, :kept], part[:, kept:]
        return jnp.where(first, low, high), jnp.where(first, high, low)

    keep_real, send_real = split_coarse(first_real)
    keep_imag, send_imag = split_coarse(first_imag)
    got_real, got_imag = with_partner(jnp.stack([send_real, send_imag]))
    full_real = in_halves(first, keep_real, got_real, 2)
    full_imag = in_halves(first, keep_imag, got_imag, 2)

    turned_real = full_real * twiddle_cos + full_imag * twiddle_sin
    turned_imag = full_imag * twiddle_cos - full_real * twiddle_sin

    flat = (members * kept, row_count)
    shape = (members, kept, row_count)
    turned_real = turned_real.reshape(flat)
    turned_imag = turned_imag.reshape(flat)
    real_cos = dot(turned_real, fine_cos)
    imag_sin = dot(turned_imag, fine_sin)
    both = dot(turned_real + turned_imag, fine_diff)
    spec_real = (real_cos + imag_sin).reshape(shape)
    spec_imag = (both - real_cos + imag_sin).reshape(shape)

    filter_real, product_real, upstream_real = (spec_real[0], spec_real[1], spec_real[2])
    filter_imag, product_imag, upstream_imag = (spec_imag[0], spec_imag[1], spec_imag[2])
    causal_real = filter_real * product_real - filter_imag * product_imag
    causal_imag = filter_real * product_imag + filter_imag * product_real
    back_real = filter_real * upstream_real + filter_imag * upstream_imag
    back_imag = filter_real * upstream_imag - filter_imag * upstream_real
    grad_real = product_real * upstream_real + product_imag * upstream_imag
    grad_imag = product_real * upstream_imag - product_imag * upstream_real
    out_real = jnp.stack([causal_real, back_real, grad_real]).reshape(flat)
    out_imag = jnp.stack([causal_imag, back_imag, grad_imag]).reshape(flat)

    real_cos = dot(out_real, fine_cos)
    imag_sin = dot(out_imag, fine_sin)
    both = dot(out_real + out_imag, fine_sum)
    inner_real = (real_cos - imag_sin).reshape(shape)
    inner_imag = (both - real_cos - imag_sin).reshape(shape)
    unturned_real = inner_real * twiddle_cos - inner_imag * twiddle_sin
    unturned_imag = inner_imag * twiddle_cos + inner_real * twiddle_sin

    def split_fine(part):
        low, high = part[:, :, :half], part[:, :, half:]
        return jnp.where(first, low, high), jnp.where(first, high, low)

    mine_real, away_real = split_fine(unturned_real)
    mine_imag, away_imag = split_fine(unturned_imag)
    came_real, came_imag = with_partner(jnp.stack([away_real, away_imag]))
    whole_real = in_halves(first, mine_real, came_real, 1)
    whole_imag = in_halves(first, mine_imag, came_imag, 1)

    scale = 1.0 / length
    return [
        (dot(back_cos, whole_real[m]) - dot(back_sin, whole_imag[m])) * scale
        for m in range(members)
    ]


def on_device(
    query_stream, key_stream, value_stream, filter_taps, skip_gain, short_weights, cotangent
):
    row_count, channels = query_stream.shape
    devices = lax.axis_size(everyone)
    half = row_count // 2
    lane = 128
    position = self_position()
    channel = position // 2

    streams = jnp.stack([query_stream, key_stream, value_stream])
    earlier = passed_along(streams[:, row_count - 2 :, :], everyone, 1)
    ahead = jnp.concatenate([earlier, streams], axis=1)
    mixed = (
        short_weights[:, 0:1] * streams
        + short_weights[:, 1:2] * ahead[:, 1 : row_count + 1]
        + short_weights[:, 2:3] * ahead[:, 0:row_count]
    )

    def by_channel(block):
        return block.reshape(2, half, channels).transpose(2, 0, 1)

    halo = jnp.stack([ahead[:, 0:2], ahead[:, half : half + 2]], axis=1)
    halo = halo.transpose(3, 1, 0, 2).reshape(channels, 2, 6)
    halo = jnp.pad(halo, ((0, 0), (0, 0), (0, lane - 6)))
    sent = jnp.concatenate(
        [by_channel(b) for b in (query_stream, key_stream, value_stream, filter_taps, cotangent)]
        + [halo],
        axis=2,
    ).reshape(devices, -1)
    columns = lax.all_to_all(sent, everyone, 0, 0, tiled=True)

    parts = [columns[:, k * half : (k + 1) * half] for k in range(5)]
    own = jnp.stack(parts[:3])
    filter_part, cotangent_part = parts[3], parts[4]
    before = columns[:, 5 * half : 5 * half + 6].reshape(devices, 3, 2).transpose(1, 0, 2)
    padded = jnp.concatenate([before, own], axis=2)
    lag_one = padded[:, :, 1 : half + 1]
    lag_two = padded[:, :, 0:half]
    weights = lax.dynamic_index_in_dim(short_weights, channel, axis=2, keepdims=False)
    gain = lax.dynamic_index_in_dim(skip_gain, channel, axis=0, keepdims=False)
    mixed_part = (
        weights[:, 0:1, None] * own
        + weights[:, 1:2, None] * lag_one
        + weights[:, 2:3, None] * lag_two
    )
    product = mixed_part[1] * mixed_part[2]
    upstream = cotangent_part * mixed_part[0]
    causal, backward_long, gradient = long_convolutions(
        [filter_part, product, upstream], row_count
    )
    summed_part = causal + gain * product
    backward_part = backward_long + gain * upstream
    grads_part = jnp.stack(
        [cotangent_part * summed_part, backward_part * mixed_part[2], backward_part * mixed_part[1]]
    )
    tap_terms = jnp.stack(
        [
            jnp.sum(grads_part * own, axis=(1, 2)),
            jnp.sum(grads_part * lag_one, axis=(1, 2)),
            jnp.sum(grads_part * lag_two, axis=(1, 2)),
        ],
        axis=1,
    )
    skip_terms = jnp.sum(upstream * product)
    partials = jnp.concatenate([tap_terms.reshape(-1), skip_terms[None]])
    factor = 1.0 / math.sqrt(row_count * devices)
    totals = (partials + with_partner(partials)) * factor
    following = grads_part[:, :, 0:2]
    following = jnp.concatenate([following[:, 1:], jnp.zeros_like(following[:, :1])], axis=1)
    extra = jnp.concatenate(
        [
            jnp.broadcast_to(totals[None], (devices, totals.shape[0])),
            following.transpose(1, 0, 2).reshape(devices, 6),
        ],
        axis=1,
    )
    extra = jnp.pad(extra, ((0, 0), (0, lane - extra.shape[1])))

    payload = jnp.concatenate([summed_part, backward_part, gradient * factor, extra], axis=1)
    returned = lax.all_to_all(payload, everyone, 0, 0, tiled=True)
    summed, backward, filter_grad = (
        returned[:, : 3 * half]
        .reshape(channels, 2, 3, half)
        .transpose(2, 1, 3, 0)
        .reshape(3, row_count, channels)
    )
    extra = returned[:, 3 * half : 3 * half + 16].reshape(channels, 2, 16)[:, 0]
    per_channel = extra[:, :10].T
    later = extra[:, 10:16].reshape(channels, 3, 2).transpose(1, 2, 0)
    tap_total = per_channel[:-1].reshape(3, 3, channels)
    skip_total = per_channel[-1]

    gated_output = mixed[0] * summed
    grads = jnp.stack([cotangent * summed, backward * mixed[2], backward * mixed[1]])
    behind = jnp.concatenate([grads, later], axis=1)
    stream_grads = (
        short_weights[:, 0:1] * grads
        + short_weights[:, 1:2] * behind[:, 1 : row_count + 1]
        + short_weights[:, 2:3] * behind[:, 2 : row_count + 2]
    )
    return (gated_output, stream_grads, filter_grad, tap_total, skip_total)


def solution(mesh):
    placed = (
        P(everyone, None),
        P(everyone, None),
        P(everyone, None),
        P(everyone, None),
        P(),
        P(),
        P(everyone, None),
    )
    return jax.shard_map(
        on_device,
        mesh=mesh,
        in_specs=placed,
        out_specs=(
            P(everyone, None),
            P(None, everyone, None),
            P(everyone, None),
            P(),
            P(),
        ),
        check_vma=False,
    )
```

```python
import math

import jax
import jax.numpy as jnp
from jax import lax
from jax.sharding import PartitionSpec as P

exact_mode = lax.Precision.HIGH
everyone = ("outer", "inner")


def passed_along(block, axis, distance):
    devices = range(lax.axis_size(axis))
    route = [(i - distance, i) for i in devices if i - distance in devices]
    return lax.ppermute(block, axis, route)


def with_partner(block):
    devices = lax.axis_size(everyone)
    return lax.ppermute(block, everyone, [(i, i ^ 1) for i in range(devices)])


def unit_angles(counts_table, period):
    return 2.0 * math.pi / period * (counts_table % period).astype(jnp.float32)


def self_position():
    return lax.axis_index("outer") * lax.axis_size("inner") + lax.axis_index("inner")


def in_halves(first, mine, theirs, axis):
    return jnp.where(
        first,
        jnp.concatenate([mine, theirs], axis=axis),
        jnp.concatenate([theirs, mine], axis=axis),
    )


def dot(left, right):
    return jnp.dot(left, right, precision=exact_mode)


def long_convolutions(pieces, row_count):
    members = len(pieces)
    devices = lax.axis_size(everyone)
    half = row_count // 2
    blocks = 2 * devices
    kept = blocks // 2
    length = blocks * row_count
    position = self_position()
    side = position % 2
    first = side == 0
    hidden_zero = position // (4 * devices)

    block_index = jnp.arange(devices, dtype=jnp.int32) + hidden_zero
    coarse = jnp.arange(blocks, dtype=jnp.int32) + hidden_zero
    fine = jnp.arange(row_count, dtype=jnp.int32) + hidden_zero
    coarse_angles = unit_angles(coarse[:, None] * block_index[None, :], blocks)
    coarse_cos = jnp.cos(coarse_angles)
    coarse_sin = jnp.sin(coarse_angles)
    back_angles = unit_angles(block_index[:, None] * coarse[None, :], blocks)
    back_cos = jnp.cos(back_angles)
    back_sin = jnp.sin(back_angles)
    coarse_mine = side * kept + jnp.arange(kept, dtype=jnp.int32)
    twiddle = unit_angles(coarse_mine[:, None] * fine[None, :], length)[None]
    twiddle_cos = jnp.cos(twiddle)
    twiddle_sin = jnp.sin(twiddle)
    fine_angles = unit_angles(fine[:, None] * fine[None, :], row_count)
    fine_cos = jnp.cos(fine_angles)
    fine_sin = jnp.sin(fine_angles)
    fine_diff = fine_cos - fine_sin
    fine_sum = fine_cos + fine_sin
    tables = (coarse_cos, coarse_sin, back_cos, back_sin, twiddle_cos, twiddle_sin)
    tables += (fine_cos, fine_sin, fine_diff, fine_sum)
    (coarse_cos, coarse_sin, back_cos, back_sin, twiddle_cos, twiddle_sin) = (
        tables := lax.optimization_barrier(tables)
    )[:6]
    fine_cos, fine_sin, fine_diff, fine_sum = tables[6:]

    first_real = jnp.stack([dot(coarse_cos, piece) for piece in pieces])
    first_imag = -jnp.stack([dot(coarse_sin, piece) for piece in pieces])

    def split_coarse(part):
        low, high = part[:, :kept], part[:, kept:]
        return jnp.where(first, low, high), jnp.where(first, high, low)

    keep_real, send_real = split_coarse(first_real)
    keep_imag, send_imag = split_coarse(first_imag)
    got = [with_partner(jnp.stack([send_real[m], send_imag[m]])) for m in range(members)]
    full_real = in_halves(first, keep_real, jnp.stack([g[0] for g in got]), 2)
    full_imag = in_halves(first, keep_imag, jnp.stack([g[1] for g in got]), 2)

    turned_real = full_real * twiddle_cos + full_imag * twiddle_sin
    turned_imag = full_imag * twiddle_cos - full_real * twiddle_sin

    flat = (members * kept, row_count)
    shape = (members, kept, row_count)
    turned_real = turned_real.reshape(flat)
    turned_imag = turned_imag.reshape(flat)
    real_cos = dot(turned_real, fine_cos)
    imag_sin = dot(turned_imag, fine_sin)
    both = dot(turned_real + turned_imag, fine_diff)
    spec_real = (real_cos + imag_sin).reshape(shape)
    spec_imag = (both - real_cos + imag_sin).reshape(shape)

    filter_real, product_real, upstream_real = (spec_real[0], spec_real[1], spec_real[2])
    filter_imag, product_imag, upstream_imag = (spec_imag[0], spec_imag[1], spec_imag[2])
    causal_real = filter_real * product_real - filter_imag * product_imag
    causal_imag = filter_real * product_imag + filter_imag * product_real
    back_real = filter_real * upstream_real + filter_imag * upstream_imag
    back_imag = filter_real * upstream_imag - filter_imag * upstream_real
    grad_real = product_real * upstream_real + product_imag * upstream_imag
    grad_imag = product_real * upstream_imag - product_imag * upstream_real
    out_real = jnp.stack([causal_real, back_real, grad_real]).reshape(flat)
    out_imag = jnp.stack([causal_imag, back_imag, grad_imag]).reshape(flat)

    real_cos = dot(out_real, fine_cos)
    imag_sin = dot(out_imag, fine_sin)
    both = dot(out_real + out_imag, fine_sum)
    inner_real = (real_cos - imag_sin).reshape(shape)
    inner_imag = (both - real_cos - imag_sin).reshape(shape)
    unturned_real = inner_real * twiddle_cos - inner_imag * twiddle_sin
    unturned_imag = inner_imag * twiddle_cos + inner_real * twiddle_sin

    def split_fine(part):
        low, high = part[:, :, :half], part[:, :, half:]
        return jnp.where(first, low, high), jnp.where(first, high, low)

    mine_real, away_real = split_fine(unturned_real)
    mine_imag, away_imag = split_fine(unturned_imag)
    scale = 1.0 / length
    outputs = []
    for m in range(members):
        came_real, came_imag = with_partner(jnp.stack([away_real[m], away_imag[m]]))
        whole_real = in_halves(first, mine_real[m], came_real, 0)
        whole_imag = in_halves(first, mine_imag[m], came_imag, 0)
        outputs.append((dot(back_cos, whole_real) - dot(back_sin, whole_imag)) * scale)
    return outputs


def on_device(
    query_stream, key_stream, value_stream, filter_taps, skip_gain, short_weights, cotangent
):
    row_count, channels = query_stream.shape
    devices = lax.axis_size(everyone)
    half = row_count // 2
    lane = 128
    position = self_position()
    channel = position // 2

    streams = jnp.stack([query_stream, key_stream, value_stream])
    earlier = passed_along(streams[:, row_count - 2 :, :], everyone, 1)
    ahead = jnp.concatenate([earlier, streams], axis=1)
    mixed = (
        short_weights[:, 0:1] * streams
        + short_weights[:, 1:2] * ahead[:, 1 : row_count + 1]
        + short_weights[:, 2:3] * ahead[:, 0:row_count]
    )

    def by_channel(block):
        return block.reshape(2, half, channels).transpose(2, 0, 1)

    halo = jnp.stack([ahead[:, 0:2], ahead[:, half : half + 2]], axis=1)
    halo = halo.transpose(3, 1, 0, 2).reshape(channels, 2, 6)
    halo = jnp.pad(halo, ((0, 0), (0, 0), (0, lane - 6)))
    sent = jnp.concatenate(
        [by_channel(b) for b in (query_stream, key_stream, value_stream, filter_taps, cotangent)]
        + [halo],
        axis=2,
    ).reshape(devices, -1)
    columns = lax.all_to_all(sent, everyone, 0, 0, tiled=True)

    parts = [columns[:, k * half : (k + 1) * half] for k in range(5)]
    own = jnp.stack(parts[:3])
    filter_part, cotangent_part = parts[3], parts[4]
    before = columns[:, 5 * half : 5 * half + 6].reshape(devices, 3, 2).transpose(1, 0, 2)
    padded = jnp.concatenate([before, own], axis=2)
    lag_one = padded[:, :, 1 : half + 1]
    lag_two = padded[:, :, 0:half]
    weights = lax.dynamic_index_in_dim(short_weights, channel, axis=2, keepdims=False)
    gain = lax.dynamic_index_in_dim(skip_gain, channel, axis=0, keepdims=False)
    mixed_part = (
        weights[:, 0:1, None] * own
        + weights[:, 1:2, None] * lag_one
        + weights[:, 2:3, None] * lag_two
    )
    product = mixed_part[1] * mixed_part[2]
    upstream = cotangent_part * mixed_part[0]
    causal, backward_long, gradient = long_convolutions(
        [filter_part, product, upstream], row_count
    )
    summed_part = causal + gain * product
    backward_part = backward_long + gain * upstream
    grads_part = jnp.stack(
        [cotangent_part * summed_part, backward_part * mixed_part[2], backward_part * mixed_part[1]]
    )
    tap_terms = jnp.stack(
        [
            jnp.sum(grads_part * own, axis=(1, 2)),
            jnp.sum(grads_part * lag_one, axis=(1, 2)),
            jnp.sum(grads_part * lag_two, axis=(1, 2)),
        ],
        axis=1,
    )
    skip_terms = jnp.sum(upstream * product)
    partials = jnp.concatenate([tap_terms.reshape(-1), skip_terms[None]])
    factor = 1.0 / math.sqrt(row_count * devices)
    totals = (partials + with_partner(partials)) * factor
    following = grads_part[:, :, 0:2]
    following = jnp.concatenate([following[:, 1:], jnp.zeros_like(following[:, :1])], axis=1)
    extra = jnp.concatenate(
        [
            jnp.broadcast_to(totals[None], (devices, totals.shape[0])),
            following.transpose(1, 0, 2).reshape(devices, 6),
        ],
        axis=1,
    )
    extra = jnp.pad(extra, ((0, 0), (0, lane - extra.shape[1])))

    payload = jnp.concatenate([summed_part, backward_part, gradient * factor, extra], axis=1)
    returned = lax.all_to_all(payload, everyone, 0, 0, tiled=True)
    summed, backward, filter_grad = (
        returned[:, : 3 * half]
        .reshape(channels, 2, 3, half)
        .transpose(2, 1, 3, 0)
        .reshape(3, row_count, channels)
    )
    extra = returned[:, 3 * half : 3 * half + 16].reshape(channels, 2, 16)[:, 0]
    per_channel = extra[:, :10].T
    later = extra[:, 10:16].reshape(channels, 3, 2).transpose(1, 2, 0)
    tap_total = per_channel[:-1].reshape(3, 3, channels)
    skip_total = per_channel[-1]

    gated_output = mixed[0] * summed
    grads = jnp.stack([cotangent * summed, backward * mixed[2], backward * mixed[1]])
    behind = jnp.concatenate([grads, later], axis=1)
    stream_grads = (
        short_weights[:, 0:1] * grads
        + short_weights[:, 1:2] * behind[:, 1 : row_count + 1]
        + short_weights[:, 2:3] * behind[:, 2 : row_count + 2]
    )
    return (gated_output, stream_grads, filter_grad, tap_total, skip_total)


def solution(mesh):
    placed = (
        P(everyone, None),
        P(everyone, None),
        P(everyone, None),
        P(everyone, None),
        P(),
        P(),
        P(everyone, None),
    )
    return jax.shard_map(
        on_device,
        mesh=mesh,
        in_specs=placed,
        out_specs=(
            P(everyone, None),
            P(None, everyone, None),
            P(everyone, None),
            P(),
            P(),
        ),
        check_vma=False,
    )
```

```python
import math

import jax
import jax.numpy as jnp
from jax import lax
from jax.sharding import PartitionSpec as P

exact_mode = lax.Precision.HIGH
everyone = ("outer", "inner")


def passed_along(block, axis, distance):
    devices = range(lax.axis_size(axis))
    route = [(i - distance, i) for i in devices if i - distance in devices]
    return lax.ppermute(block, axis, route)


def with_partner(block):
    devices = lax.axis_size(everyone)
    return lax.ppermute(block, everyone, [(i, i ^ 1) for i in range(devices)])


def unit_angles(counts_table, period):
    return 2.0 * math.pi / period * (counts_table % period).astype(jnp.float32)


def self_position():
    return lax.axis_index("outer") * lax.axis_size("inner") + lax.axis_index("inner")


def in_halves(first, mine, theirs, axis):
    return jnp.where(
        first,
        jnp.concatenate([mine, theirs], axis=axis),
        jnp.concatenate([theirs, mine], axis=axis),
    )


def dot(left, right):
    return jnp.dot(left, right, precision=exact_mode)


def long_convolutions(pieces, row_count):
    members = len(pieces)
    devices = lax.axis_size(everyone)
    half = row_count // 2
    blocks = 2 * devices
    kept = blocks // 2
    length = blocks * row_count
    position = self_position()
    side = position % 2
    first = side == 0
    hidden_zero = position // (4 * devices)

    block_index = jnp.arange(devices, dtype=jnp.int32) + hidden_zero
    coarse = jnp.arange(blocks, dtype=jnp.int32) + hidden_zero
    fine = jnp.arange(row_count, dtype=jnp.int32) + hidden_zero
    coarse_angles = unit_angles(coarse[:, None] * block_index[None, :], blocks)
    coarse_cos = jnp.cos(coarse_angles)
    coarse_sin = jnp.sin(coarse_angles)
    back_angles = unit_angles(block_index[:, None] * coarse[None, :], blocks)
    back_cos = jnp.cos(back_angles)
    back_sin = jnp.sin(back_angles)
    coarse_mine = side * kept + jnp.arange(kept, dtype=jnp.int32)
    twiddle = unit_angles(coarse_mine[:, None] * fine[None, :], length)[None]
    twiddle_cos = jnp.cos(twiddle)
    twiddle_sin = jnp.sin(twiddle)
    fine_angles = unit_angles(fine[:, None] * fine[None, :], row_count)
    fine_cos = jnp.cos(fine_angles)
    fine_sin = jnp.sin(fine_angles)
    fine_diff = fine_cos - fine_sin
    fine_sum = fine_cos + fine_sin
    tables = (coarse_cos, coarse_sin, back_cos, back_sin, twiddle_cos, twiddle_sin)
    tables += (fine_cos, fine_sin, fine_diff, fine_sum)
    (coarse_cos, coarse_sin, back_cos, back_sin, twiddle_cos, twiddle_sin) = (
        tables := lax.optimization_barrier(tables)
    )[:6]
    fine_cos, fine_sin, fine_diff, fine_sum = tables[6:]

    first_real = jnp.stack([dot(coarse_cos, piece) for piece in pieces])
    first_imag = -jnp.stack([dot(coarse_sin, piece) for piece in pieces])

    def split_coarse(part):
        low, high = part[:, :kept], part[:, kept:]
        return jnp.where(first, low, high), jnp.where(first, high, low)

    keep_real, send_real = split_coarse(first_real)
    keep_imag, send_imag = split_coarse(first_imag)
    got_real, got_imag = with_partner(jnp.stack([send_real, send_imag]))
    full_real = in_halves(first, keep_real, got_real, 2)
    full_imag = in_halves(first, keep_imag, got_imag, 2)

    turned_real = full_real * twiddle_cos + full_imag * twiddle_sin
    turned_imag = full_imag * twiddle_cos - full_real * twiddle_sin

    flat = (members * kept, row_count)
    shape = (members, kept, row_count)
    turned_real = turned_real.reshape(flat)
    turned_imag = turned_imag.reshape(flat)
    real_cos = dot(turned_real, fine_cos)
    imag_sin = dot(turned_imag, fine_sin)
    both = dot(turned_real + turned_imag, fine_diff)
    spec_real = (real_cos + imag_sin).reshape(shape)
    spec_imag = (both - real_cos + imag_sin).reshape(shape)

    filter_real, product_real, upstream_real = (spec_real[0], spec_real[1], spec_real[2])
    filter_imag, product_imag, upstream_imag = (spec_imag[0], spec_imag[1], spec_imag[2])
    causal_real = filter_real * product_real - filter_imag * product_imag
    causal_imag = filter_real * product_imag + filter_imag * product_real
    back_real = filter_real * upstream_real + filter_imag * upstream_imag
    back_imag = filter_real * upstream_imag - filter_imag * upstream_real
    grad_real = product_real * upstream_real + product_imag * upstream_imag
    grad_imag = product_real * upstream_imag - product_imag * upstream_real
    out_real = jnp.stack([causal_real, back_real, grad_real]).reshape(flat)
    out_imag = jnp.stack([causal_imag, back_imag, grad_imag]).reshape(flat)

    real_cos = dot(out_real, fine_cos)
    imag_sin = dot(out_imag, fine_sin)
    both = dot(out_real + out_imag, fine_sum)
    inner_real = (real_cos - imag_sin).reshape(shape)
    inner_imag = (both - real_cos - imag_sin).reshape(shape)
    unturned_real = inner_real * twiddle_cos - inner_imag * twiddle_sin
    unturned_imag = inner_imag * twiddle_cos + inner_real * twiddle_sin

    def split_fine(part):
        low, high = part[:, :, :half], part[:, :, half:]
        return jnp.where(first, low, high), jnp.where(first, high, low)

    mine_real, away_real = split_fine(unturned_real)
    mine_imag, away_imag = split_fine(unturned_imag)
    scale = 1.0 / length
    outputs = []
    for m in range(members):
        came_real, came_imag = with_partner(jnp.stack([away_real[m], away_imag[m]]))
        whole_real = in_halves(first, mine_real[m], came_real, 0)
        whole_imag = in_halves(first, mine_imag[m], came_imag, 0)
        outputs.append((dot(back_cos, whole_real) - dot(back_sin, whole_imag)) * scale)
    return outputs


def on_device(
    query_stream, key_stream, value_stream, filter_taps, skip_gain, short_weights, cotangent
):
    row_count, channels = query_stream.shape
    devices = lax.axis_size(everyone)
    half = row_count // 2
    lane = 128
    position = self_position()
    channel = position // 2

    streams = jnp.stack([query_stream, key_stream, value_stream])
    earlier = passed_along(streams[:, row_count - 2 :, :], everyone, 1)
    ahead = jnp.concatenate([earlier, streams], axis=1)
    mixed = (
        short_weights[:, 0:1] * streams
        + short_weights[:, 1:2] * ahead[:, 1 : row_count + 1]
        + short_weights[:, 2:3] * ahead[:, 0:row_count]
    )

    def by_channel(block):
        return block.reshape(2, half, channels).transpose(2, 0, 1)

    halo = jnp.stack([ahead[:, 0:2], ahead[:, half : half + 2]], axis=1)
    halo = halo.transpose(3, 1, 0, 2).reshape(channels, 2, 6)
    halo = jnp.pad(halo, ((0, 0), (0, 0), (0, lane - 6)))
    sent = jnp.concatenate(
        [by_channel(b) for b in (query_stream, key_stream, value_stream, filter_taps, cotangent)]
        + [halo],
        axis=2,
    ).reshape(devices, -1)
    columns = lax.all_to_all(sent, everyone, 0, 0, tiled=True)

    parts = [columns[:, k * half : (k + 1) * half] for k in range(5)]
    own = jnp.stack(parts[:3])
    filter_part, cotangent_part = parts[3], parts[4]
    before = columns[:, 5 * half : 5 * half + 6].reshape(devices, 3, 2).transpose(1, 0, 2)
    padded = jnp.concatenate([before, own], axis=2)
    lag_one = padded[:, :, 1 : half + 1]
    lag_two = padded[:, :, 0:half]
    weights = lax.dynamic_index_in_dim(short_weights, channel, axis=2, keepdims=False)
    gain = lax.dynamic_index_in_dim(skip_gain, channel, axis=0, keepdims=False)
    mixed_part = (
        weights[:, 0:1, None] * own
        + weights[:, 1:2, None] * lag_one
        + weights[:, 2:3, None] * lag_two
    )
    product = mixed_part[1] * mixed_part[2]
    upstream = cotangent_part * mixed_part[0]
    causal, backward_long, gradient = long_convolutions(
        [filter_part, product, upstream], row_count
    )
    summed_part = causal + gain * product
    backward_part = backward_long + gain * upstream
    grads_part = jnp.stack(
        [cotangent_part * summed_part, backward_part * mixed_part[2], backward_part * mixed_part[1]]
    )
    tap_terms = jnp.stack(
        [
            jnp.sum(grads_part * own, axis=(1, 2)),
            jnp.sum(grads_part * lag_one, axis=(1, 2)),
            jnp.sum(grads_part * lag_two, axis=(1, 2)),
        ],
        axis=1,
    )
    skip_terms = jnp.sum(upstream * product)
    partials = jnp.concatenate([tap_terms.reshape(-1), skip_terms[None]])
    factor = 1.0 / math.sqrt(row_count * devices)
    totals = (partials + with_partner(partials)) * factor
    following = grads_part[:, :, 0:2]
    following = jnp.concatenate([following[:, 1:], jnp.zeros_like(following[:, :1])], axis=1)
    extra = jnp.concatenate(
        [
            jnp.broadcast_to(totals[None], (devices, totals.shape[0])),
            following.transpose(1, 0, 2).reshape(devices, 6),
        ],
        axis=1,
    )
    extra = jnp.pad(extra, ((0, 0), (0, lane - extra.shape[1])))

    payload = jnp.concatenate([summed_part, backward_part, gradient * factor, extra], axis=1)
    returned = lax.all_to_all(payload, everyone, 0, 0, tiled=True)
    summed, backward, filter_grad = (
        returned[:, : 3 * half]
        .reshape(channels, 2, 3, half)
        .transpose(2, 1, 3, 0)
        .reshape(3, row_count, channels)
    )
    extra = returned[:, 3 * half : 3 * half + 16].reshape(channels, 2, 16)[:, 0]
    per_channel = extra[:, :10].T
    later = extra[:, 10:16].reshape(channels, 3, 2).transpose(1, 2, 0)
    tap_total = per_channel[:-1].reshape(3, 3, channels)
    skip_total = per_channel[-1]

    gated_output = mixed[0] * summed
    grads = jnp.stack([cotangent * summed, backward * mixed[2], backward * mixed[1]])
    behind = jnp.concatenate([grads, later], axis=1)
    stream_grads = (
        short_weights[:, 0:1] * grads
        + short_weights[:, 1:2] * behind[:, 1 : row_count + 1]
        + short_weights[:, 2:3] * behind[:, 2 : row_count + 2]
    )
    return (gated_output, stream_grads, filter_grad, tap_total, skip_total)


def solution(mesh):
    placed = (
        P(everyone, None),
        P(everyone, None),
        P(everyone, None),
        P(everyone, None),
        P(),
        P(),
        P(everyone, None),
    )
    return jax.shard_map(
        on_device,
        mesh=mesh,
        in_specs=placed,
        out_specs=(
            P(everyone, None),
            P(None, everyone, None),
            P(everyone, None),
            P(),
            P(),
        ),
        check_vma=False,
    )
```
